256 devices in a mesh: blk: 32 (over x, y, core), sub: 8 (over z).
Axes of the slice: x: 4, y: 4, z: 8, core: 2. Of those that a mesh axis runs over, the one named last changes fastest.
Arguments:
- block_vec: bfloat16 [64, 512, 512], P('blk', 'sub'), may hold values from -6 to 6
- left_factor: bfloat16 [8, 512, 512], replicated, may hold values from -0.25 to 0.25
- right_factor: bfloat16 [8, 512, 512], replicated, may hold values from -0.25 to 0.25
- pairs: int32 [32, 32, 2, 3], replicated, may hold values from 0 to 7, as said below
- pair_count: int32 [32, 32], replicated, may hold values from 1 to 2, as said below
- left_basis: bfloat16 [64, 512, 512], P('blk'), may hold values from -0.25 to 0.25
- left_dual: bfloat16 [64, 512, 512], P('blk'), may hold values from -0.25 to 0.25
- right_eigenvector_matrix: bfloat16 [64, 512, 512], P('blk'), may hold values from -0.25 to 0.25
- right_dual: bfloat16 [64, 512, 512], P('blk'), may hold values from -0.25 to 0.25
- left_rates: float32 [64, 512], P('blk', 'sub'), may hold values from 0.5 to 8
- right_rates: float32 [64, 512], P('blk'), may hold values from 0.5 to 8
Outputs:
- next_vec: float32 [64, 512, 512], P('blk', None, 'sub')
The draws below stay inside these ranges and needn't reach their ends.
Inputs may be any that keep to these rules, and one draw needn't show every extreme that they name: `pairs`: entry [g, h, c, 0] is a source block index within group g, [g, h, c, 1] a target block index within group h (0 to 1), and [g, h, c, 2] a term index (0 to 7); where g equals h, source and target differ. For some target group h, pair_count[g, h] is 2 for every g.
All inputs are finite; a program needn't handle non-finite values.
Results may differ from the reference program's by a relative error of at most 0.023.
Values may be sent and summed in bfloat16 or wider, within the bound.
No kernel may reach another device: no remote copies, remote signals or barrier semaphores. Data moves between devices by JAX's collectives and lax.ppermute only.
A program may use at most 64 MiB of HBM per device.

```python
import math
import jax
import jax.numpy as jnp
from jax import lax

N1 = 512
N2 = 512
TERMS = 8
BPG = 2
CAP = 2
GROUPS = 32
NBLK = 64


def draw_pairs(key, part):
    random_key_parts = jax.random.split(key, 4)
    slot_shape = (GROUPS, GROUPS, CAP)
    source_local = jax.random.randint(random_key_parts[0], slot_shape, 0, BPG)
    target_other = jax.random.randint(random_key_parts[1], slot_shape, 0, BPG)
    offset = jax.random.randint(random_key_parts[2], slot_shape, 1, BPG)
    term_id = jax.random.randint(random_key_parts[3], slot_shape, 0, TERMS)
    same_group = jnp.arange(GROUPS)[:, None, None] == jnp.arange(GROUPS)[None, :, None]
    target_local = jnp.where(same_group, (source_local + offset) % BPG, target_other)
    return jnp.stack([source_local, target_local, term_id], axis=-1).astype(jnp.int32)


def draw_pair_count(key, part):
    key_one, key_two = jax.random.split(key)
    counts = jax.random.randint(key_one, (GROUPS, GROUPS), 1, CAP + 1)
    busiest = jax.random.randint(key_two, (), 0, GROUPS)
    return jnp.where(jnp.arange(GROUPS)[None, :] == busiest, CAP, counts).astype(jnp.int32)


def level_of(key, extent, cuts, smallest, high):
    level, own = 1.0, jax.random.fold_in(key, 6)
    for dim, blocks in cuts:
        draws = jnp.exp(jax.random.uniform(jax.random.fold_in(own, dim), (blocks,), jnp.float32, smallest / len(cuts), high / len(cuts)))
        level = level * jnp.repeat(draws, extent[dim] // blocks).reshape([-1 if axis == dim else 1 for axis in range(len(extent))])
    return level


def noise(key, dims, width, most, cuts=(), held_as=jnp.bfloat16):
    entries = width * jax.random.normal(key, dims, jnp.float32)
    if cuts:
        entries = entries * level_of(key, dims, cuts, -0.22, 0.18)
    return jnp.clip(entries, -most, most).astype(held_as)


def setup_inputs(seed: int = 0) -> dict:
    splits = jax.random.split(jax.random.key(seed), 12)
    block_vec = noise(splits[0], (NBLK, N1, N2), 1.0, 6.0, ((0, 32), (1, 8)))
    left_factor = noise(splits[1], (TERMS, N1, N1), N1 ** -0.5, 0.25)
    right_factor = noise(splits[2], (TERMS, N2, N2), N2 ** -0.5, 0.25)
    pairs = draw_pairs(jax.random.fold_in(splits[11], 71), 0)
    pair_count = draw_pair_count(jax.random.fold_in(splits[11], 71), 0)
    left_basis = noise(splits[5], (NBLK, N1, N1), N1 ** -0.5, 0.25, ((0, 32),))
    left_dual = noise(splits[6], (NBLK, N1, N1), N1 ** -0.5, 0.25, ((0, 32),))
    right_eigenvector_matrix = noise(splits[7], (NBLK, N2, N2), N2 ** -0.5, 0.25, ((0, 32),))
    right_dual = noise(splits[8], (NBLK, N2, N2), N2 ** -0.5, 0.25, ((0, 32),))
    left_rates = jnp.clip(jnp.exp(math.log(8.0) - 2.7725887 * jax.random.uniform(splits[9], (NBLK, N1), jnp.float32) ** level_of(splits[9], (NBLK, N1), ((0, 32), (1, 8)), -0.2, 0.2)), 0.5, 8.0)
    right_rates = jnp.clip(jnp.exp(math.log(8.0) - 2.7725887 * jax.random.uniform(splits[10], (NBLK, N2), jnp.float32) ** level_of(splits[10], (NBLK, N2), ((0, 32),), -0.2, 0.2)), 0.5, 8.0)
    return dict(block_vec=block_vec, left_factor=left_factor, right_factor=right_factor, pairs=pairs, pair_count=pair_count, left_basis=left_basis, left_dual=left_dual, right_eigenvector_matrix=right_eigenvector_matrix, right_dual=right_dual, left_rates=left_rates, right_rates=right_rates)


def reference(block_vec, left_factor, right_factor, pairs, pair_count, left_basis, left_dual, right_eigenvector_matrix, right_dual, left_rates, right_rates):
    left_wide = left_factor.astype(jnp.float32)
    right_wide = right_factor.astype(jnp.float32)
    vectors_wide = block_vec.astype(jnp.float32)
    group_count = pair_count.shape[0]
    source = jnp.arange(group_count, dtype=jnp.int32)[:, None, None] * BPG + pairs[..., 0]
    target = jnp.arange(group_count, dtype=jnp.int32)[None, :, None] * BPG + pairs[..., 1]
    target_term = target * TERMS + pairs[..., 2]
    live_mask = (jnp.arange(CAP, dtype=jnp.int32)[None, None, :] < pair_count[:, :, None]).astype(jnp.float32)
    weights = jnp.zeros((NBLK * TERMS, NBLK), jnp.float32)
    weights = weights.at[target_term.reshape(-1), source.reshape(-1)].add(live_mask.reshape(-1))
    weights = weights.reshape(NBLK, TERMS, NBLK)

    def gather_block(weight_one):
        pooled = jnp.einsum("ts,sab->tab", weight_one, vectors_wide).astype(jnp.bfloat16)
        right_done = jnp.einsum("tan,tmn->tam", pooled.astype(jnp.float32), right_wide).astype(jnp.bfloat16)
        return jnp.einsum("tfq,tqp->fp", left_wide, right_done.astype(jnp.float32)).astype(jnp.bfloat16)

    summed = lax.map(gather_block, weights)

    def solve_block(block_items):
        summed_one, basis_one, dual_one, second_eigenbasis, dual_two, rates_one, rates_two = block_items
        dual_cols = jnp.dot(dual_one, summed_one, preferred_element_type=jnp.float32).astype(jnp.bfloat16)
        mixed = jnp.dot(dual_cols, dual_two.T, preferred_element_type=jnp.float32)
        scaled = (mixed / (rates_one[:, None] + rates_two[None, :])).astype(jnp.bfloat16)
        basis_rows = jnp.dot(scaled, second_eigenbasis.T, preferred_element_type=jnp.float32).astype(jnp.bfloat16)
        return jnp.dot(basis_one, basis_rows, preferred_element_type=jnp.float32)

    return lax.map(solve_block, (summed, left_basis, left_dual, right_eigenvector_matrix, right_dual, left_rates, right_rates))
```

```python
import jax
import jax.numpy as jnp
from jax import lax
from jax.sharding import PartitionSpec as P


def local(
    block_vec,
    left_factor,
    right_factor,
    pairs,
    pair_count,
    left_basis,
    left_dual,
    right_eigenvector_matrix,
    right_dual,
    left_rates,
    right_rates,
):
    owner = lax.axis_index("blk")
    part = lax.axis_index("sub")
    groups = lax.axis_size("blk")
    local_blocks = block_vec.shape[0]
    row_count = block_vec.shape[1]
    width_two = block_vec.shape[2]
    slots_per = pairs.shape[2]
    term_total = left_factor.shape[0]
    all_count = groups * local_blocks
    next_cols = width_two // lax.axis_size("sub")
    incoming = lax.dynamic_index_in_dim(pairs, owner, 1, keepdims=False)
    counts = lax.dynamic_index_in_dim(pair_count, owner, 1, keepdims=False)
    live_mask = (jnp.arange(slots_per)[None, :] < counts[:, None]).astype(jnp.float32)
    target_term = incoming[..., 1] * term_total + incoming[..., 2]
    source = jnp.arange(groups, dtype=jnp.int32)[:, None] * local_blocks + incoming[..., 0]
    key_onehot = (
        target_term[..., None] == jnp.arange(local_blocks * term_total)[None, None, :]
    ).astype(jnp.float32) * live_mask[..., None]
    source_onehot = (source[..., None] == jnp.arange(all_count)[None, None, :]).astype(jnp.float32)
    weights = jnp.einsum("gqk,gqs->ks", key_onehot, source_onehot).astype(jnp.bfloat16)
    rates_full = lax.all_gather(left_rates, "sub", axis=1, tiled=True)
    everything = lax.all_gather(block_vec, "blk", axis=0, tiled=True)
    pooled = jnp.einsum(
        "ks,srn->krn", weights, everything, preferred_element_type=jnp.float32
    ).astype(jnp.bfloat16)
    pooled = pooled.reshape(local_blocks, term_total, row_count, width_two)
    right_done = jnp.einsum(
        "ktrn,tmn->ktrm", pooled, right_factor, preferred_element_type=jnp.float32
    ).astype(jnp.bfloat16)
    left_part = lax.dynamic_slice_in_dim(left_factor, part * row_count, row_count, axis=2)
    partial = jnp.einsum(
        "tab,ktbc->kac", left_part, right_done, preferred_element_type=jnp.float32
    ).astype(jnp.bfloat16)
    summed = lax.psum(partial, "sub")
    dual_cols = jnp.einsum(
        "jab,jbc->jac", left_dual, summed, preferred_element_type=jnp.float32
    ).astype(jnp.bfloat16)
    mixed = jnp.einsum("jrn,jmn->jrm", dual_cols, right_dual, preferred_element_type=jnp.float32)
    scaled = (mixed / (rates_full[:, :, None] + right_rates[:, None, :])).astype(jnp.bfloat16)
    eig_part = lax.dynamic_slice_in_dim(right_eigenvector_matrix, part * next_cols, next_cols, axis=1)
    basis_cols = jnp.einsum(
        "jrm,jkm->jrk", scaled, eig_part, preferred_element_type=jnp.float32
    ).astype(jnp.bfloat16)
    return jnp.einsum("jab,jbc->jac", left_basis, basis_cols, preferred_element_type=jnp.float32)


def solution(mesh):
    placed = (
        P("blk", "sub", None),
        P(),
        P(),
        P(),
        P(),
        P("blk", None, None),
        P("blk", None, None),
        P("blk", None, None),
        P("blk", None, None),
        P("blk", "sub"),
        P("blk", None),
    )
    return jax.shard_map(
        local, mesh=mesh, in_specs=placed, out_specs=P("blk", None, "sub"), check_vma=False
    )
```

```python
import jax
import jax.numpy as jnp
from jax import lax
from jax.sharding import PartitionSpec as P


def exchange(chunks, axis):
    n = chunks.shape[0]
    me = lax.axis_index(axis)
    out = jnp.zeros_like(chunks)
    own = lax.dynamic_index_in_dim(chunks, me, 0, keepdims=True)
    out = lax.dynamic_update_index_in_dim(out, own, me, 0)
    for k in range(1, n):
        send = lax.dynamic_index_in_dim(chunks, (me + k) % n, 0, keepdims=True)
        got = lax.ppermute(send, axis, [(j, (j + k) % n) for j in range(n)])
        out = lax.dynamic_update_index_in_dim(out, got, (me - k) % n, 0)
    return out


def local(
    block_vec,
    left_factor,
    right_factor,
    pairs,
    pair_count,
    left_basis,
    left_dual,
    right_eigenvector_matrix,
    right_dual,
    left_rates,
    right_rates,
):
    owner = lax.axis_index("blk")
    part = lax.axis_index("sub")
    groups = lax.axis_size("blk")
    pieces = lax.axis_size("sub")
    local_blocks = block_vec.shape[0]
    row_count = block_vec.shape[1]
    width_two = block_vec.shape[2]
    slots_per = pairs.shape[2]
    term_total = left_factor.shape[0]
    all_count = groups * local_blocks
    cols = width_two // pieces
    incoming = lax.dynamic_index_in_dim(pairs, owner, 1, keepdims=False)
    counts = lax.dynamic_index_in_dim(pair_count, owner, 1, keepdims=False)
    live_mask = (jnp.arange(slots_per)[None, :] < counts[:, None]).astype(jnp.float32)
    target_term = incoming[..., 1] * term_total + incoming[..., 2]
    source = jnp.arange(groups, dtype=jnp.int32)[:, None] * local_blocks + incoming[..., 0]
    key_onehot = (
        target_term[..., None] == jnp.arange(local_blocks * term_total)[None, None, :]
    ).astype(jnp.float32) * live_mask[..., None]
    source_onehot = (source[..., None] == jnp.arange(all_count)[None, None, :]).astype(jnp.float32)
    weights = jnp.einsum("gqk,gqs->ks", key_onehot, source_onehot).astype(jnp.bfloat16)
    everything = lax.all_gather(block_vec, "blk", axis=0, tiled=True)
    pooled = jnp.einsum(
        "ks,srn->krn", weights, everything, preferred_element_type=jnp.float32
    ).astype(jnp.bfloat16)
    pooled = pooled.reshape(local_blocks, term_total, row_count, width_two)
    right_done = jnp.einsum(
        "ktrn,tmn->ktrm", pooled, right_factor, preferred_element_type=jnp.float32
    ).astype(jnp.bfloat16)
    right_done = right_done.reshape(local_blocks, term_total, row_count, pieces, cols)
    left_part = lax.dynamic_slice_in_dim(left_factor, part * row_count, row_count, axis=2)
    partial = jnp.einsum(
        "tab,ktbjc->jkac", left_part, right_done, preferred_element_type=jnp.float32
    ).astype(jnp.bfloat16)
    gathered = exchange(partial, "sub")
    summed = jnp.sum(gathered.astype(jnp.float32), axis=0).astype(jnp.bfloat16)
    dual_cols = jnp.einsum(
        "jab,jbc->jac", left_dual, summed, preferred_element_type=jnp.float32
    ).astype(jnp.bfloat16)
    dual_chunks = jnp.moveaxis(dual_cols.reshape(local_blocks, pieces, row_count, cols), 1, 0)
    dual_rows = exchange(dual_chunks, "sub")
    dual_rows = jnp.moveaxis(dual_rows, 0, 2).reshape(local_blocks, row_count, width_two)
    mixed = jnp.einsum("jrn,jmn->jrm", dual_rows, right_dual, preferred_element_type=jnp.float32)
    scaled = (mixed / (left_rates[:, :, None] + right_rates[:, None, :])).astype(jnp.bfloat16)
    basis_rows = jnp.einsum(
        "jrm,jkm->jrk", scaled, right_eigenvector_matrix, preferred_element_type=jnp.float32
    ).astype(jnp.bfloat16)
    basis_chunks = jnp.moveaxis(basis_rows.reshape(local_blocks, row_count, pieces, cols), 2, 0)
    basis_cols = exchange(basis_chunks, "sub")
    basis_cols = jnp.moveaxis(basis_cols, 0, 1).reshape(local_blocks, width_two, cols)
    return jnp.einsum("jab,jbc->jac", left_basis, basis_cols, preferred_element_type=jnp.float32)


def solution(mesh):
    placed = (
        P("blk", "sub", None),
        P(),
        P(),
        P(),
        P(),
        P("blk", None, None),
        P("blk", None, None),
        P("blk", None, None),
        P("blk", None, None),
        P("blk", "sub"),
        P("blk", None),
    )
    return jax.shard_map(
        local, mesh=mesh, in_specs=placed, out_specs=P("blk", None, "sub"), check_vma=False
    )
```

```python
import jax
import jax.numpy as jnp
from jax import lax
from jax.sharding import PartitionSpec as P


def exchange(chunks, axis):
    n = chunks.shape[0]
    me = lax.axis_index(axis)
    out = jnp.zeros_like(chunks)
    own = lax.dynamic_index_in_dim(chunks, me, 0, keepdims=True)
    out = lax.dynamic_update_index_in_dim(out, own, me, 0)
    for k in range(1, n):
        send = lax.dynamic_index_in_dim(chunks, (me + k) % n, 0, keepdims=True)
        got = lax.ppermute(send, axis, [(j, (j + k) % n) for j in range(n)])
        out = lax.dynamic_update_index_in_dim(out, got, (me - k) % n, 0)
    return out


def scatter_sum(chunks, axis):
    n = chunks.shape[0]
    me = lax.axis_index(axis)
    total = lax.dynamic_index_in_dim(chunks, me, 0, keepdims=False).astype(jnp.float32)
    for k in range(1, n):
        send = lax.dynamic_index_in_dim(chunks, (me + k) % n, 0, keepdims=False)
        got = lax.ppermute(send, axis, [(j, (j + k) % n) for j in range(n)])
        total = total + got.astype(jnp.float32)
    return total


def local(
    block_vec,
    left_factor,
    right_factor,
    pairs,
    pair_count,
    left_basis,
    left_dual,
    right_eigenvector_matrix,
    right_dual,
    left_rates,
    right_rates,
):
    owner = lax.axis_index("blk")
    part = lax.axis_index("sub")
    groups = lax.axis_size("blk")
    pieces = lax.axis_size("sub")
    local_blocks = block_vec.shape[0]
    row_count = block_vec.shape[1]
    width_two = block_vec.shape[2]
    slots_per = pairs.shape[2]
    term_total = left_factor.shape[0]
    all_count = groups * local_blocks
    cols = width_two // pieces
    incoming = lax.dynamic_index_in_dim(pairs, owner, 1, keepdims=False)
    counts = lax.dynamic_index_in_dim(pair_count, owner, 1, keepdims=False)
    live_mask = (jnp.arange(slots_per)[None, :] < counts[:, None]).astype(jnp.float32)
    target_term = incoming[..., 1] * term_total + incoming[..., 2]
    source = jnp.arange(groups, dtype=jnp.int32)[:, None] * local_blocks + incoming[..., 0]
    key_onehot = (
        target_term[..., None] == jnp.arange(local_blocks * term_total)[None, None, :]
    ).astype(jnp.float32) * live_mask[..., None]
    source_onehot = (source[..., None] == jnp.arange(all_count)[None, None, :]).astype(jnp.float32)
    weights = jnp.einsum("gqk,gqs->ks", key_onehot, source_onehot).astype(jnp.bfloat16)
    everything = lax.all_gather(block_vec, "blk", axis=0, tiled=True)
    pooled = jnp.einsum(
        "ks,srn->krn", weights, everything, preferred_element_type=jnp.float32
    ).astype(jnp.bfloat16)
    pooled = pooled.reshape(local_blocks, term_total, row_count, width_two)
    right_done = jnp.einsum(
        "ktrn,tmn->ktrm", pooled, right_factor, preferred_element_type=jnp.float32
    ).astype(jnp.bfloat16)
    left_part = lax.dynamic_slice_in_dim(left_factor, part * row_count, row_count, axis=2)
    rates_parts = exchange(jnp.broadcast_to(left_rates, (pieces,) + left_rates.shape), "sub")
    rates_full = jnp.moveaxis(rates_parts, 0, 1).reshape(local_blocks, width_two)
    partial = jnp.einsum(
        "tab,ktbc->kac", left_part, right_done, preferred_element_type=jnp.float32
    ).astype(jnp.bfloat16)
    dual_cols = jnp.einsum(
        "jab,jbc->jac", left_dual, partial, preferred_element_type=jnp.float32
    ).astype(jnp.bfloat16)
    mixed = jnp.einsum("jrn,jmn->jrm", dual_cols, right_dual, preferred_element_type=jnp.float32)
    scaled = (mixed / (rates_full[:, :, None] + right_rates[:, None, :])).astype(jnp.bfloat16)
    basis_rows = jnp.einsum(
        "jrm,jkm->jrk", scaled, right_eigenvector_matrix, preferred_element_type=jnp.float32
    ).astype(jnp.bfloat16)
    basis_rows = basis_rows.reshape(local_blocks, width_two, pieces, cols)
    spread = jnp.einsum(
        "jab,jbkc->kjac", left_basis, basis_rows, preferred_element_type=jnp.float32
    ).astype(jnp.bfloat16)
    return scatter_sum(spread, "sub")


def solution(mesh):
    placed = (
        P("blk", "sub", None),
        P(),
        P(),
        P(),
        P(),
        P("blk", None, None),
        P("blk", None, None),
        P("blk", None, None),
        P("blk", None, None),
        P("blk", "sub"),
        P("blk", None),
    )
    return jax.shard_map(
        local, mesh=mesh, in_specs=placed, out_specs=P("blk", None, "sub"), check_vma=False
    )
```

```python
import jax
import jax.numpy as jnp
from jax import lax
from jax.sharding import PartitionSpec as P


def exchange(chunks, axis):
    n = chunks.shape[0]
    me = lax.axis_index(axis)
    out = jnp.zeros_like(chunks)
    own = lax.dynamic_index_in_dim(chunks, me, 0, keepdims=True)
    out = lax.dynamic_update_index_in_dim(out, own, me, 0)
    for k in range(1, n):
        send = lax.dynamic_index_in_dim(chunks, (me + k) % n, 0, keepdims=True)
        got = lax.ppermute(send, axis, [(j, (j + k) % n) for j in range(n)])
        out = lax.dynamic_update_index_in_dim(out, got, (me - k) % n, 0)
    return out


def scatter_sum(chunks, axis):
    n = chunks.shape[0]
    me = lax.axis_index(axis)
    total = lax.dynamic_index_in_dim(chunks, me, 0, keepdims=False).astype(jnp.float32)
    for k in range(1, n):
        send = lax.dynamic_index_in_dim(chunks, (me + k) % n, 0, keepdims=False)
        got = lax.ppermute(send, axis, [(j, (j + k) % n) for j in range(n)])
        total = total + got.astype(jnp.float32)
    return total


def local(
    block_vec,
    left_factor,
    right_factor,
    pairs,
    pair_count,
    left_basis,
    left_dual,
    right_eigenvector_matrix,
    right_dual,
    left_rates,
    right_rates,
):
    owner = lax.axis_index("blk")
    part = lax.axis_index("sub")
    groups = lax.axis_size("blk")
    pieces = lax.axis_size("sub")
    local_blocks = block_vec.shape[0]
    row_count = block_vec.shape[1]
    width_two = block_vec.shape[2]
    slots_per = pairs.shape[2]
    term_total = left_factor.shape[0]
    all_count = groups * local_blocks
    cols = width_two // pieces
    incoming = lax.dynamic_index_in_dim(pairs, owner, 1, keepdims=False)
    counts = lax.dynamic_index_in_dim(pair_count, owner, 1, keepdims=False)
    live_mask = (jnp.arange(slots_per)[None, :] < counts[:, None]).astype(jnp.float32)
    target_term = incoming[..., 1] * term_total + incoming[..., 2]
    source = jnp.arange(groups, dtype=jnp.int32)[:, None] * local_blocks + incoming[..., 0]
    key_onehot = (
        target_term[..., None] == jnp.arange(local_blocks * term_total)[None, None, :]
    ).astype(jnp.float32) * live_mask[..., None]
    core = owner % 2
    half_index = jnp.arange(all_count // 2, dtype=jnp.int32)
    mine_ids = ((half_index // local_blocks) * 2 + core) * local_blocks + half_index % local_blocks
    other_ids = ((half_index // local_blocks) * 2 + 1 - core) * local_blocks + half_index % local_blocks
    mine_onehot = (source[..., None] == mine_ids[None, None, :]).astype(jnp.float32)
    other_onehot = (source[..., None] == other_ids[None, None, :]).astype(jnp.float32)
    weights_mine = jnp.einsum("gqk,gqs->ks", key_onehot, mine_onehot).astype(jnp.bfloat16)
    weights_other = jnp.einsum("gqk,gqs->ks", key_onehot, other_onehot).astype(jnp.bfloat16)
    same_core = [[j for j in range(groups) if j % 2 == r] for r in range(2)]
    half = lax.all_gather(block_vec, "blk", axis=0, tiled=True, axis_index_groups=same_core)
    other = lax.ppermute(half, "blk", [(j, j ^ 1) for j in range(groups)])
    pooled = (
        jnp.einsum("ks,srn->krn", weights_mine, half, preferred_element_type=jnp.float32)
        + jnp.einsum("ks,srn->krn", weights_other, other, preferred_element_type=jnp.float32)
    ).astype(jnp.bfloat16)
    pooled = pooled.reshape(local_blocks, term_total, row_count, width_two)
    right_done = jnp.einsum(
        "ktrn,tmn->ktrm", pooled, right_factor, preferred_element_type=jnp.float32
    ).astype(jnp.bfloat16)
    left_part = lax.dynamic_slice_in_dim(left_factor, part * row_count, row_count, axis=2)
    rates_parts = exchange(jnp.broadcast_to(left_rates, (pieces,) + left_rates.shape), "sub")
    rates_full = jnp.moveaxis(rates_parts, 0, 1).reshape(local_blocks, width_two)
    partial = jnp.einsum(
        "tab,ktbc->kac", left_part, right_done, preferred_element_type=jnp.float32
    ).astype(jnp.bfloat16)
    dual_cols = jnp.einsum(
        "jab,jbc->jac", left_dual, partial, preferred_element_type=jnp.float32
    ).astype(jnp.bfloat16)
    mixed = jnp.einsum("jrn,jmn->jrm", dual_cols, right_dual, preferred_element_type=jnp.float32)
    scaled = (mixed / (rates_full[:, :, None] + right_rates[:, None, :])).astype(jnp.bfloat16)
    basis_rows = jnp.einsum(
        "jrm,jkm->jrk", scaled, right_eigenvector_matrix, preferred_element_type=jnp.float32
    ).astype(jnp.bfloat16)
    basis_rows = basis_rows.reshape(local_blocks, width_two, pieces, cols)
    spread = jnp.einsum(
        "jab,jbkc->kjac", left_basis, basis_rows, preferred_element_type=jnp.float32
    ).astype(jnp.bfloat16)
    return scatter_sum(spread, "sub")


def solution(mesh):
    placed = (
        P("blk", "sub", None),
        P(),
        P(),
        P(),
        P(),
        P("blk", None, None),
        P("blk", None, None),
        P("blk", None, None),
        P("blk", None, None),
        P("blk", "sub"),
        P("blk", None),
    )
    return jax.shard_map(
        local, mesh=mesh, in_specs=placed, out_specs=P("blk", None, "sub"), check_vma=False
    )
```

```python
import jax
import jax.numpy as jnp
from jax import lax
from jax.sharding import PartitionSpec as P


def exchange(chunks, axis):
    n = chunks.shape[0]
    me = lax.axis_index(axis)
    out = jnp.zeros_like(chunks)
    own = lax.dynamic_index_in_dim(chunks, me, 0, keepdims=True)
    out = lax.dynamic_update_index_in_dim(out, own, me, 0)
    for k in range(1, n):
        send = lax.dynamic_index_in_dim(chunks, (me + k) % n, 0, keepdims=True)
        got = lax.ppermute(send, axis, [(j, (j + k) % n) for j in range(n)])
        out = lax.dynamic_update_index_in_dim(out, got, (me - k) % n, 0)
    return out


def scatter_sum(chunks, axis):
    n = chunks.shape[0]
    me = lax.axis_index(axis)
    total = lax.dynamic_index_in_dim(chunks, me, 0, keepdims=False).astype(jnp.float32)
    for k in range(1, n):
        send = lax.dynamic_index_in_dim(chunks, (me + k) % n, 0, keepdims=False)
        got = lax.ppermute(send, axis, [(j, (j + k) % n) for j in range(n)])
        total = total + got.astype(jnp.float32)
    return total


def local(
    block_vec,
    left_factor,
    right_factor,
    pairs,
    pair_count,
    left_basis,
    left_dual,
    right_eigenvector_matrix,
    right_dual,
    left_rates,
    right_rates,
):
    owner = lax.axis_index("blk")
    part = lax.axis_index("sub")
    groups = lax.axis_size("blk")
    pieces = lax.axis_size("sub")
    local_blocks = block_vec.shape[0]
    row_count = block_vec.shape[1]
    width_two = block_vec.shape[2]
    slots_per = pairs.shape[2]
    term_total = left_factor.shape[0]
    all_count = groups * local_blocks
    cols = width_two // pieces
    incoming = lax.dynamic_index_in_dim(pairs, owner, 1, keepdims=False)
    counts = lax.dynamic_index_in_dim(pair_count, owner, 1, keepdims=False)
    live_mask = (jnp.arange(slots_per)[None, :] < counts[:, None]).astype(jnp.float32)
    target_term = incoming[..., 1] * term_total + incoming[..., 2]
    source = jnp.arange(groups, dtype=jnp.int32)[:, None] * local_blocks + incoming[..., 0]
    key_onehot = (
        target_term[..., None] == jnp.arange(local_blocks * term_total)[None, None, :]
    ).astype(jnp.float32) * live_mask[..., None]
    ring = 4
    core = owner % 2
    here_x = owner // (2 * ring)
    here_y = (owner // 2) % ring
    offsets = jnp.arange(ring, dtype=jnp.int32)
    plane_group = (((here_x + offsets[None, :]) % ring) * ring + (here_y + offsets[:, None]) % ring) * 2
    side_group = plane_group[None] + jnp.stack([core, 1 - core])[:, None, None]
    block_ids = (side_group[..., None] * local_blocks + jnp.arange(local_blocks)).reshape(-1)
    source_onehot = (source[..., None] == block_ids[None, None, :]).astype(jnp.float32)
    weights = jnp.einsum("gqk,gqs->ks", key_onehot, source_onehot).astype(jnp.bfloat16)
    weights = weights.reshape(local_blocks * term_total, 2, ring, ring, local_blocks)

    def move(piece, dx, dy, sibling=False):
        pairs_list = []
        for b in range(groups):
            bx, by, bc = b // (2 * ring), (b // 2) % ring, b % 2
            if sibling:
                dest = b ^ 1
            else:
                dest = (((bx + dx) % ring) * ring + (by + dy) % ring) * 2 + bc
            pairs_list.append((b, dest))
        return lax.ppermute(piece, "blk", pairs_list)

    half_rows = row_count // 2
    from_left = move(block_vec, 1, 0)
    from_right = move(block_vec, -1, 0)
    far = jnp.concatenate(
        [move(from_left[:, :half_rows], 1, 0), move(from_right[:, half_rows:], -1, 0)], axis=1
    )
    x_row = jnp.stack([block_vec, from_right, far, from_left])
    from_below = move(x_row, 0, 1)
    from_above = move(x_row, 0, -1)
    far_y = jnp.concatenate(
        [move(from_below[:, :, :half_rows], 0, 1), move(from_above[:, :, half_rows:], 0, -1)], axis=2
    )
    plane = jnp.stack([x_row, from_above, far_y, from_below])
    other = move(plane, 0, 0, sibling=True)

    def pool(w, piece):
        return jnp.einsum("kab,abrn->krn", w, piece, preferred_element_type=jnp.float32)

    pooled = (
        pool(weights[:, 0, 0], x_row)
        + pool(weights[:, 0, 1], from_above)
        + pool(weights[:, 0, 2], far_y)
        + pool(weights[:, 0, 3], from_below)
        + jnp.einsum(
            "kyab,yabrn->krn", weights[:, 1], other, preferred_element_type=jnp.float32
        )
    ).astype(jnp.bfloat16)
    pooled = pooled.reshape(local_blocks, term_total, row_count, width_two)
    right_done = jnp.einsum(
        "ktrn,tmn->ktrm", pooled, right_factor, preferred_element_type=jnp.float32
    ).astype(jnp.bfloat16)
    left_part = lax.dynamic_slice_in_dim(left_factor, part * row_count, row_count, axis=2)
    rates_parts = exchange(jnp.broadcast_to(left_rates, (pieces,) + left_rates.shape), "sub")
    rates_full = jnp.moveaxis(rates_parts, 0, 1).reshape(local_blocks, width_two)
    partial = jnp.einsum(
        "tab,ktbc->kac", left_part, right_done, preferred_element_type=jnp.float32
    ).astype(jnp.bfloat16)
    dual_cols = jnp.einsum(
        "jab,jbc->jac", left_dual, partial, preferred_element_type=jnp.float32
    ).astype(jnp.bfloat16)
    mixed = jnp.einsum("jrn,jmn->jrm", dual_cols, right_dual, preferred_element_type=jnp.float32)
    scaled = (mixed / (rates_full[:, :, None] + right_rates[:, None, :])).astype(jnp.bfloat16)
    basis_rows = jnp.einsum(
        "jrm,jkm->jrk", scaled, right_eigenvector_matrix, preferred_element_type=jnp.float32
    ).astype(jnp.bfloat16)
    basis_rows = basis_rows.reshape(local_blocks, width_two, pieces, cols)
    spread = jnp.einsum(
        "jab,jbkc->kjac", left_basis, basis_rows, preferred_element_type=jnp.float32
    ).astype(jnp.bfloat16)
    return scatter_sum(spread, "sub")


def solution(mesh):
    placed = (
        P("blk", "sub", None),
        P(),
        P(),
        P(),
        P(),
        P("blk", None, None),
        P("blk", None, None),
        P("blk", None, None),
        P("blk", None, None),
        P("blk", "sub"),
        P("blk", None),
    )
    return jax.shard_map(
        local, mesh=mesh, in_specs=placed, out_specs=P("blk", None, "sub"), check_vma=False
    )
```

```python
import jax
import jax.numpy as jnp
from jax import lax
from jax.sharding import PartitionSpec as P


def scatter_sum(chunks, axis):
    n = chunks.shape[0]
    me = lax.axis_index(axis)
    total = lax.dynamic_index_in_dim(chunks, me, 0, keepdims=False).astype(jnp.float32)
    for k in range(1, n):
        send = lax.dynamic_index_in_dim(chunks, (me + k) % n, 0, keepdims=False)
        got = lax.ppermute(send, axis, [(j, (j + k) % n) for j in range(n)])
        total = total + got.astype(jnp.float32)
    return total


def local(
    block_vec,
    left_factor,
    right_factor,
    pairs,
    pair_count,
    left_basis,
    left_dual,
    right_eigenvector_matrix,
    right_dual,
    left_rates,
    right_rates,
):
    owner = lax.axis_index("blk")
    part = lax.axis_index("sub")
    groups = lax.axis_size("blk")
    pieces = lax.axis_size("sub")
    local_blocks = block_vec.shape[0]
    row_count = block_vec.shape[1]
    width_two = block_vec.shape[2]
    slots_per = pairs.shape[2]
    term_total = left_factor.shape[0]
    all_count = groups * local_blocks
    cols = width_two // pieces
    incoming = lax.dynamic_index_in_dim(pairs, owner, 1, keepdims=False)
    counts = lax.dynamic_index_in_dim(pair_count, owner, 1, keepdims=False)
    live_mask = (jnp.arange(slots_per)[None, :] < counts[:, None]).astype(jnp.float32)
    target_term = incoming[..., 1] * term_total + incoming[..., 2]
    source = jnp.arange(groups, dtype=jnp.int32)[:, None] * local_blocks + incoming[..., 0]
    key_onehot = (
        target_term[..., None] == jnp.arange(local_blocks * term_total)[None, None, :]
    ).astype(jnp.float32) * live_mask[..., None]
    ring = 4
    core = owner % 2
    here_x = owner // (2 * ring)
    here_y = (owner // 2) % ring
    offsets = jnp.arange(ring, dtype=jnp.int32)
    plane_group = (((here_x + offsets[None, :]) % ring) * ring + (here_y + offsets[:, None]) % ring) * 2
    side_group = plane_group[None] + jnp.stack([core, 1 - core])[:, None, None]
    block_ids = (side_group[..., None] * local_blocks + jnp.arange(local_blocks)).reshape(-1)
    source_onehot = (source[..., None] == block_ids[None, None, :]).astype(jnp.float32)
    weights = jnp.einsum("gqk,gqs->ks", key_onehot, source_onehot).astype(jnp.bfloat16)
    weights = weights.reshape(local_blocks * term_total, 2, ring, ring, local_blocks)

    def move(piece, dx, dy, sibling=False):
        pairs_list = []
        for b in range(groups):
            bx, by, bc = b // (2 * ring), (b // 2) % ring, b % 2
            if sibling:
                dest = b ^ 1
            else:
                dest = (((bx + dx) % ring) * ring + (by + dy) % ring) * 2 + bc
            pairs_list.append((b, dest))
        return lax.ppermute(piece, "blk", pairs_list)

    half_blocks = local_blocks // 2
    from_left = move(block_vec, 1, 0)
    from_right = move(block_vec, -1, 0)
    far = jnp.concatenate(
        [move(from_left[:half_blocks], 1, 0), move(from_right[half_blocks:], -1, 0)], axis=0
    )
    x_row = jnp.stack([block_vec, from_right, far, from_left])
    side_x = move(x_row, 0, 0, sibling=True)
    from_below = move(x_row, 0, 1)
    from_above = move(x_row, 0, -1)
    side_above = move(from_above, 0, 0, sibling=True)
    side_below = move(from_below, 0, 0, sibling=True)
    half_ring = ring // 2
    far_y = jnp.concatenate(
        [move(from_below[:half_ring], 0, 1), move(from_above[half_ring:], 0, -1)], axis=0
    )
    side_far = move(far_y, 0, 0, sibling=True)

    def pool(w, piece):
        return jnp.einsum("kab,abrn->krn", w, piece, preferred_element_type=jnp.float32)

    pooled = (
        pool(weights[:, 0, 0], x_row)
        + pool(weights[:, 0, 1], from_above)
        + pool(weights[:, 0, 2], far_y)
        + pool(weights[:, 0, 3], from_below)
        + pool(weights[:, 1, 0], side_x)
        + pool(weights[:, 1, 1], side_above)
        + pool(weights[:, 1, 2], side_far)
        + pool(weights[:, 1, 3], side_below)
    ).astype(jnp.bfloat16)
    pooled = pooled.reshape(local_blocks, term_total, row_count, width_two)
    right_done = jnp.einsum(
        "ktrn,tmn->ktrm", pooled, right_factor, preferred_element_type=jnp.float32
    ).astype(jnp.bfloat16)
    left_part = lax.dynamic_slice_in_dim(left_factor, part * row_count, row_count, axis=2)
    rates_run = left_rates[None]
    step = 1
    while step < pieces:
        came = lax.ppermute(rates_run, "sub", [(j, (j + step) % pieces) for j in range(pieces)])
        rates_run = jnp.concatenate([came, rates_run], axis=0)
        step *= 2
    rates_twice = jnp.concatenate([rates_run, rates_run], axis=0)
    rates_parts = lax.dynamic_slice_in_dim(rates_twice, (pieces - 1 - part) % pieces, pieces, axis=0)
    rates_full = jnp.moveaxis(rates_parts, 0, 1).reshape(local_blocks, width_two)
    partial = jnp.einsum(
        "tab,ktbc->kac", left_part, right_done, preferred_element_type=jnp.float32
    ).astype(jnp.bfloat16)
    dual_cols = jnp.einsum(
        "jab,jbc->jac", left_dual, partial, preferred_element_type=jnp.float32
    ).astype(jnp.bfloat16)
    mixed = jnp.einsum("jrn,jmn->jrm", dual_cols, right_dual, preferred_element_type=jnp.float32)
    scaled = (mixed / (rates_full[:, :, None] + right_rates[:, None, :])).astype(jnp.bfloat16)
    basis_rows = jnp.einsum(
        "jrm,jkm->jrk", scaled, right_eigenvector_matrix, preferred_element_type=jnp.float32
    ).astype(jnp.bfloat16)
    basis_rows = basis_rows.reshape(local_blocks, width_two, pieces, cols)
    spread = jnp.einsum(
        "jab,jbkc->kjac", left_basis, basis_rows, preferred_element_type=jnp.float32
    ).astype(jnp.bfloat16)
    return scatter_sum(spread, "sub")


def solution(mesh):
    placed = (
        P("blk", "sub", None),
        P(),
        P(),
        P(),
        P(),
        P("blk", None, None),
        P("blk", None, None),
        P("blk", None, None),
        P("blk", None, None),
        P("blk", "sub"),
        P("blk", None),
    )
    return jax.shard_map(
        local, mesh=mesh, in_specs=placed, out_specs=P("blk", None, "sub"), check_vma=False
    )
```

```python
import jax
import jax.numpy as jnp
from jax import lax
from jax.sharding import PartitionSpec as P


def scatter_sum(chunks, axis):
    n = chunks.shape[0]
    me = lax.axis_index(axis)
    total = lax.dynamic_index_in_dim(chunks, me, 0, keepdims=False).astype(jnp.float32)
    for k in range(1, n):
        send = lax.dynamic_index_in_dim(chunks, (me + k) % n, 0, keepdims=False)
        got = lax.ppermute(send, axis, [(j, (j + k) % n) for j in range(n)])
        total = total + got.astype(jnp.float32)
    return total


def local(
    block_vec,
    left_factor,
    right_factor,
    pairs,
    pair_count,
    left_basis,
    left_dual,
    right_eigenvector_matrix,
    right_dual,
    left_rates,
    right_rates,
):
    owner = lax.axis_index("blk")
    part = lax.axis_index("sub")
    groups = lax.axis_size("blk")
    pieces = lax.axis_size("sub")
    local_blocks = block_vec.shape[0]
    row_count = block_vec.shape[1]
    width_two = block_vec.shape[2]
    slots_per = pairs.shape[2]
    term_total = left_factor.shape[0]
    all_count = groups * local_blocks
    cols = width_two // pieces
    incoming = lax.dynamic_index_in_dim(pairs, owner, 1, keepdims=False)
    counts = lax.dynamic_index_in_dim(pair_count, owner, 1, keepdims=False)
    live_mask = (jnp.arange(slots_per)[None, :] < counts[:, None]).astype(jnp.float32)
    target_term = incoming[..., 1] * term_total + incoming[..., 2]
    source = jnp.arange(groups, dtype=jnp.int32)[:, None] * local_blocks + incoming[..., 0]
    key_onehot = (
        target_term[..., None] == jnp.arange(local_blocks * term_total)[None, None, :]
    ).astype(jnp.float32) * live_mask[..., None]
    ring = 4
    core = owner % 2
    here_x = owner // (2 * ring)
    here_y = (owner // 2) % ring
    offsets = jnp.arange(ring, dtype=jnp.int32)
    plane_group = (((here_x + offsets[None, :]) % ring) * ring + (here_y + offsets[:, None]) % ring) * 2
    side_group = plane_group[None] + jnp.stack([core, 1 - core])[:, None, None]
    block_ids = (side_group[..., None] * local_blocks + jnp.arange(local_blocks)).reshape(-1)
    source_onehot = (source[..., None] == block_ids[None, None, :]).astype(jnp.float32)
    weights = jnp.einsum("gqk,gqs->ks", key_onehot, source_onehot).astype(jnp.bfloat16)
    weights = weights.reshape(local_blocks * term_total, 2, ring, ring, local_blocks)

    def move(piece, dx, dy, sibling=False):
        pairs_list = []
        for b in range(groups):
            bx, by, bc = b // (2 * ring), (b // 2) % ring, b % 2
            if sibling:
                dest = b ^ 1
            else:
                dest = (((bx + dx) % ring) * ring + (by + dy) % ring) * 2 + bc
            pairs_list.append((b, dest))
        return lax.ppermute(piece, "blk", pairs_list)

    half_blocks = local_blocks // 2
    from_left = move(block_vec, 1, 0)
    from_right = move(block_vec, -1, 0)
    far = jnp.concatenate(
        [move(from_left[:half_blocks], 1, 0), move(from_right[half_blocks:], -1, 0)], axis=0
    )
    x_row = jnp.stack([block_vec, from_right, far, from_left])
    side_x = move(x_row, 0, 0, sibling=True)
    from_below = move(x_row, 0, 1)
    from_above = move(x_row, 0, -1)
    side_above = move(from_above, 0, 0, sibling=True)
    side_below = move(from_below, 0, 0, sibling=True)
    half_ring = ring // 2
    far_y = jnp.concatenate(
        [move(from_below[:half_ring], 0, 1), move(from_above[half_ring:], 0, -1)], axis=0
    )
    side_far = move(far_y, 0, 0, sibling=True)

    def pool(w, piece):
        return jnp.einsum("kab,abrn->krn", w, piece, preferred_element_type=jnp.float32)

    pooled = (
        pool(weights[:, 0, 0], x_row)
        + pool(weights[:, 0, 1], from_above)
        + pool(weights[:, 0, 2], far_y)
        + pool(weights[:, 0, 3], from_below)
        + pool(weights[:, 1, 0], side_x)
        + pool(weights[:, 1, 1], side_above)
        + pool(weights[:, 1, 2], side_far)
        + pool(weights[:, 1, 3], side_below)
    ).astype(jnp.bfloat16)
    pooled = pooled.reshape(local_blocks, term_total, row_count, width_two)
    right_done = jnp.einsum(
        "ktrn,tmn->ktrm", pooled, right_factor, preferred_element_type=jnp.float32
    ).astype(jnp.bfloat16)
    left_part = lax.dynamic_slice_in_dim(left_factor, part * row_count, row_count, axis=2)
    rates_run, pooled = lax.optimization_barrier((left_rates[None], pooled))
    step = 1
    while step < pieces:
        came = lax.ppermute(rates_run, "sub", [(j, (j + step) % pieces) for j in range(pieces)])
        rates_run = jnp.concatenate([came, rates_run], axis=0)
        step *= 2
    rates_twice = jnp.concatenate([rates_run, rates_run], axis=0)
    rates_parts = lax.dynamic_slice_in_dim(rates_twice, (pieces - 1 - part) % pieces, pieces, axis=0)
    rates_full = jnp.moveaxis(rates_parts, 0, 1).reshape(local_blocks, width_two)
    partial = jnp.einsum(
        "tab,ktbc->kac", left_part, right_done, preferred_element_type=jnp.float32
    ).astype(jnp.bfloat16)
    dual_cols = jnp.einsum(
        "jab,jbc->jac", left_dual, partial, preferred_element_type=jnp.float32
    ).astype(jnp.bfloat16)
    mixed = jnp.einsum("jrn,jmn->jrm", dual_cols, right_dual, preferred_element_type=jnp.float32)
    scaled = (mixed / (rates_full[:, :, None] + right_rates[:, None, :])).astype(jnp.bfloat16)
    basis_rows = jnp.einsum(
        "jrm,jkm->jrk", scaled, right_eigenvector_matrix, preferred_element_type=jnp.float32
    ).astype(jnp.bfloat16)
    basis_rows = basis_rows.reshape(local_blocks, width_two, pieces, cols)
    spread = jnp.einsum(
        "jab,jbkc->kjac", left_basis, basis_rows, preferred_element_type=jnp.float32
    ).astype(jnp.bfloat16)
    return scatter_sum(spread, "sub")


def solution(mesh):
    placed = (
        P("blk", "sub", None),
        P(),
        P(),
        P(),
        P(),
        P("blk", None, None),
        P("blk", None, None),
        P("blk", None, None),
        P("blk", None, None),
        P("blk", "sub"),
        P("blk", None),
    )
    return jax.shard_map(
        local, mesh=mesh, in_specs=placed, out_specs=P("blk", None, "sub"), check_vma=False
    )
```

```python
import jax
import jax.numpy as jnp
from jax import lax
from jax.sharding import PartitionSpec as P


def scatter_sum(chunks, axis):
    n = chunks.shape[0]
    me = lax.axis_index(axis)
    total = lax.dynamic_index_in_dim(chunks, me, 0, keepdims=False).astype(jnp.float32)
    for k in range(1, n):
        send = lax.dynamic_index_in_dim(chunks, (me + k) % n, 0, keepdims=False)
        got = lax.ppermute(send, axis, [(j, (j + k) % n) for j in range(n)])
        total = total + got.astype(jnp.float32)
    return total


def local(
    block_vec,
    left_factor,
    right_factor,
    pairs,
    pair_count,
    left_basis,
    left_dual,
    right_eigenvector_matrix,
    right_dual,
    left_rates,
    right_rates,
):
    owner = lax.axis_index("blk")
    part = lax.axis_index("sub")
    groups = lax.axis_size("blk")
    pieces = lax.axis_size("sub")
    local_blocks = block_vec.shape[0]
    row_count = block_vec.shape[1]
    width_two = block_vec.shape[2]
    slots_per = pairs.shape[2]
    term_total = left_factor.shape[0]
    all_count = groups * local_blocks
    cols = width_two // pieces
    incoming = lax.dynamic_index_in_dim(pairs, owner, 1, keepdims=False)
    counts = lax.dynamic_index_in_dim(pair_count, owner, 1, keepdims=False)
    live_mask = (jnp.arange(slots_per)[None, :] < counts[:, None]).astype(jnp.float32)
    target_term = incoming[..., 1] * term_total + incoming[..., 2]
    source = jnp.arange(groups, dtype=jnp.int32)[:, None] * local_blocks + incoming[..., 0]
    key_onehot = (
        target_term[..., None] == jnp.arange(local_blocks * term_total)[None, None, :]
    ).astype(jnp.float32) * live_mask[..., None]
    ring = 4
    core = owner % 2
    here_x = owner // (2 * ring)
    here_y = (owner // 2) % ring
    offsets = jnp.arange(ring, dtype=jnp.int32)
    plane_group = (((here_x + offsets[None, :]) % ring) * ring + (here_y + offsets[:, None]) % ring) * 2
    side_group = plane_group[None] + jnp.stack([core, 1 - core])[:, None, None]
    block_ids = (side_group[..., None] * local_blocks + jnp.arange(local_blocks)).reshape(-1)
    source_onehot = (source[..., None] == block_ids[None, None, :]).astype(jnp.float32)
    weights = jnp.einsum("gqk,gqs->ks", key_onehot, source_onehot).astype(jnp.bfloat16)
    weights = weights.reshape(local_blocks * term_total, 2, ring, ring, local_blocks)

    def move(piece, dx, dy, sibling=False):
        pairs_list = []
        for b in range(groups):
            bx, by, bc = b // (2 * ring), (b // 2) % ring, b % 2
            if sibling:
                dest = b ^ 1
            else:
                dest = (((bx + dx) % ring) * ring + (by + dy) % ring) * 2 + bc
            pairs_list.append((b, dest))
        return lax.ppermute(piece, "blk", pairs_list)

    half_blocks = local_blocks // 2
    from_left = move(block_vec, 1, 0)
    from_right = move(block_vec, -1, 0)
    far = jnp.concatenate(
        [move(from_left[:half_blocks], 1, 0), move(from_right[half_blocks:], -1, 0)], axis=0
    )
    x_row = jnp.stack([block_vec, from_right, far, from_left])
    side_x = move(x_row, 0, 0, sibling=True)
    from_below = move(x_row, 0, 1)
    from_above = move(x_row, 0, -1)
    rates_seed, from_above, from_below = lax.optimization_barrier(
        (left_rates[None], from_above, from_below)
    )
    side_above = move(from_above, 0, 0, sibling=True)
    side_below = move(from_below, 0, 0, sibling=True)
    half_ring = ring // 2
    far_y = jnp.concatenate(
        [move(from_below[:half_ring], 0, 1), move(from_above[half_ring:], 0, -1)], axis=0
    )
    side_far = move(far_y, 0, 0, sibling=True)

    def pool(w, piece):
        return jnp.einsum("kab,abrn->krn", w, piece, preferred_element_type=jnp.float32)

    pooled = (
        pool(weights[:, 0, 0], x_row)
        + pool(weights[:, 0, 1], from_above)
        + pool(weights[:, 0, 2], far_y)
        + pool(weights[:, 0, 3], from_below)
        + pool(weights[:, 1, 0], side_x)
        + pool(weights[:, 1, 1], side_above)
        + pool(weights[:, 1, 2], side_far)
        + pool(weights[:, 1, 3], side_below)
    ).astype(jnp.bfloat16)
    pooled = pooled.reshape(local_blocks, term_total, row_count, width_two)
    right_done = jnp.einsum(
        "ktrn,tmn->ktrm", pooled, right_factor, preferred_element_type=jnp.float32
    ).astype(jnp.bfloat16)
    left_part = lax.dynamic_slice_in_dim(left_factor, part * row_count, row_count, axis=2)
    rates_parts = jnp.zeros((pieces,) + left_rates.shape, left_rates.dtype)
    rates_parts = lax.dynamic_update_index_in_dim(rates_parts, rates_seed, part, 0)
    for k in range(1, pieces):
        came = lax.ppermute(rates_seed, "sub", [(j, (j + k) % pieces) for j in range(pieces)])
        rates_parts = lax.dynamic_update_index_in_dim(rates_parts, came, (part - k) % pieces, 0)
    rates_full = jnp.moveaxis(rates_parts, 0, 1).reshape(local_blocks, width_two)
    partial = jnp.einsum(
        "tab,ktbc->kac", left_part, right_done, preferred_element_type=jnp.float32
    ).astype(jnp.bfloat16)
    dual_cols = jnp.einsum(
        "jab,jbc->jac", left_dual, partial, preferred_element_type=jnp.float32
    ).astype(jnp.bfloat16)
    mixed = jnp.einsum("jrn,jmn->jrm", dual_cols, right_dual, preferred_element_type=jnp.float32)
    scaled = (mixed / (rates_full[:, :, None] + right_rates[:, None, :])).astype(jnp.bfloat16)
    basis_rows = jnp.einsum(
        "jrm,jkm->jrk", scaled, right_eigenvector_matrix, preferred_element_type=jnp.float32
    ).astype(jnp.bfloat16)
    basis_rows = basis_rows.reshape(local_blocks, width_two, pieces, cols)
    spread = jnp.einsum(
        "jab,jbkc->kjac", left_basis, basis_rows, preferred_element_type=jnp.float32
    ).astype(jnp.bfloat16)
    return scatter_sum(spread, "sub")


def solution(mesh):
    placed = (
        P("blk", "sub", None),
        P(),
        P(),
        P(),
        P(),
        P("blk", None, None),
        P("blk", None, None),
        P("blk", None, None),
        P("blk", None, None),
        P("blk", "sub"),
        P("blk", None),
    )
    return jax.shard_map(
        local, mesh=mesh, in_specs=placed, out_specs=P("blk", None, "sub"), check_vma=False
    )
```

```python
import jax
import jax.numpy as jnp
from jax import lax
from jax.sharding import PartitionSpec as P


def scatter_sum(chunks, axis):
    n = chunks.shape[0]
    me = lax.axis_index(axis)
    total = lax.dynamic_index_in_dim(chunks, me, 0, keepdims=False).astype(jnp.float32)
    for k in range(1, n):
        send = lax.dynamic_index_in_dim(chunks, (me + k) % n, 0, keepdims=False)
        got = lax.ppermute(send, axis, [(j, (j + k) % n) for j in range(n)])
        total = total + got.astype(jnp.float32)
    return total


def local(
    block_vec,
    left_factor,
    right_factor,
    pairs,
    pair_count,
    left_basis,
    left_dual,
    right_eigenvector_matrix,
    right_dual,
    left_rates,
    right_rates,
):
    owner = lax.axis_index("blk")
    part = lax.axis_index("sub")
    groups = lax.axis_size("blk")
    pieces = lax.axis_size("sub")
    local_blocks = block_vec.shape[0]
    row_count = block_vec.shape[1]
    width_two = block_vec.shape[2]
    slots_per = pairs.shape[2]
    term_total = left_factor.shape[0]
    all_count = groups * local_blocks
    cols = width_two // pieces
    incoming = lax.dynamic_index_in_dim(pairs, owner, 1, keepdims=False)
    counts = lax.dynamic_index_in_dim(pair_count, owner, 1, keepdims=False)
    live_mask = (jnp.arange(slots_per)[None, :] < counts[:, None]).astype(jnp.float32)
    target_term = incoming[..., 1] * term_total + incoming[..., 2]
    source = jnp.arange(groups, dtype=jnp.int32)[:, None] * local_blocks + incoming[..., 0]
    key_onehot = (
        target_term[..., None] == jnp.arange(local_blocks * term_total)[None, None, :]
    ).astype(jnp.float32) * live_mask[..., None]
    ring = 4
    core = owner % 2
    here_x = owner // (2 * ring)
    here_y = (owner // 2) % ring
    offsets = jnp.arange(ring, dtype=jnp.int32)
    plane_group = (((here_x + offsets[None, :]) % ring) * ring + (here_y + offsets[:, None]) % ring) * 2
    side_group = plane_group[None] + jnp.stack([core, 1 - core])[:, None, None]
    block_ids = (side_group[..., None] * local_blocks + jnp.arange(local_blocks)).reshape(-1)
    source_onehot = (source[..., None] == block_ids[None, None, :]).astype(jnp.float32)
    weights = jnp.einsum("gqk,gqs->ks", key_onehot, source_onehot).astype(jnp.bfloat16)
    weights = weights.reshape(local_blocks * term_total, 2, ring, ring, local_blocks)

    def move(piece, dx, dy, sibling=False):
        pairs_list = []
        for b in range(groups):
            bx, by, bc = b // (2 * ring), (b // 2) % ring, b % 2
            if sibling:
                dest = b ^ 1
            else:
                dest = (((bx + dx) % ring) * ring + (by + dy) % ring) * 2 + bc
            pairs_list.append((b, dest))
        return lax.ppermute(piece, "blk", pairs_list)

    half_blocks = local_blocks // 2
    from_left = move(block_vec, 1, 0)
    from_right = move(block_vec, -1, 0)
    far = jnp.concatenate(
        [move(from_left[:half_blocks], 1, 0), move(from_right[half_blocks:], -1, 0)], axis=0
    )
    x_row = jnp.stack([block_vec, from_right, far, from_left])
    side_x = move(x_row, 0, 0, sibling=True)
    from_below = move(x_row, 0, 1)
    from_above = move(x_row, 0, -1)
    side_above = move(from_above, 0, 0, sibling=True)
    side_below = move(from_below, 0, 0, sibling=True)
    half_ring = ring // 2
    far_y = jnp.concatenate(
        [move(from_below[:half_ring], 0, 1), move(from_above[half_ring:], 0, -1)], axis=0
    )
    side_far = move(far_y, 0, 0, sibling=True)

    def pool(w, piece):
        return jnp.einsum("kab,abrn->krn", w, piece, preferred_element_type=jnp.float32)

    pooled = (
        pool(weights[:, 0, 0], x_row)
        + pool(weights[:, 0, 1], from_above)
        + pool(weights[:, 0, 2], far_y)
        + pool(weights[:, 0, 3], from_below)
        + pool(weights[:, 1, 0], side_x)
        + pool(weights[:, 1, 1], side_above)
        + pool(weights[:, 1, 2], side_far)
        + pool(weights[:, 1, 3], side_below)
    ).astype(jnp.bfloat16)
    pooled = pooled.reshape(local_blocks, term_total, row_count, width_two)
    right_done = jnp.einsum(
        "ktrn,tmn->ktrm", pooled, right_factor, preferred_element_type=jnp.float32
    ).astype(jnp.bfloat16)
    left_part = lax.dynamic_slice_in_dim(left_factor, part * row_count, row_count, axis=2)
    partial = jnp.einsum(
        "tab,ktbc->kac", left_part, right_done, preferred_element_type=jnp.float32
    ).astype(jnp.bfloat16)
    dual_cols = jnp.einsum(
        "jab,jbc->jac", left_dual, partial, preferred_element_type=jnp.float32
    ).astype(jnp.bfloat16)
    dual_cols = dual_cols.reshape(local_blocks, pieces, row_count, width_two)
    mixed_parts = jnp.einsum(
        "jsrn,jmn->sjrm", dual_cols, right_dual, preferred_element_type=jnp.float32
    ).astype(jnp.bfloat16)
    mixed = scatter_sum(mixed_parts, "sub")
    scaled = (mixed / (left_rates[:, :, None] + right_rates[:, None, :])).astype(jnp.bfloat16)
    basis_rows = jnp.einsum(
        "jrm,jkm->jrk", scaled, right_eigenvector_matrix, preferred_element_type=jnp.float32
    ).astype(jnp.bfloat16)
    basis_cols = lax.all_to_all(basis_rows, "sub", split_axis=2, concat_axis=1, tiled=True)
    return jnp.einsum("jab,jbc->jac", left_basis, basis_cols, preferred_element_type=jnp.float32)


def solution(mesh):
    placed = (
        P("blk", "sub", None),
        P(),
        P(),
        P(),
        P(),
        P("blk", None, None),
        P("blk", None, None),
        P("blk", None, None),
        P("blk", None, None),
        P("blk", "sub"),
        P("blk", None),
    )
    return jax.shard_map(
        local, mesh=mesh, in_specs=placed, out_specs=P("blk", None, "sub"), check_vma=False
    )
```

```python
import jax
import jax.numpy as jnp
from jax import lax
from jax.sharding import PartitionSpec as P


def scatter_sum(chunks, axis):
    n = chunks.shape[0]
    me = lax.axis_index(axis)
    total = lax.dynamic_index_in_dim(chunks, me, 0, keepdims=False).astype(jnp.float32)
    for k in range(1, n):
        send = lax.dynamic_index_in_dim(chunks, (me + k) % n, 0, keepdims=False)
        got = lax.ppermute(send, axis, [(j, (j + k) % n) for j in range(n)])
        total = total + got.astype(jnp.float32)
    return total


def local(
    block_vec,
    left_factor,
    right_factor,
    pairs,
    pair_count,
    left_basis,
    left_dual,
    right_eigenvector_matrix,
    right_dual,
    left_rates,
    right_rates,
):
    owner = lax.axis_index("blk")
    part = lax.axis_index("sub")
    groups = lax.axis_size("blk")
    pieces = lax.axis_size("sub")
    local_blocks = block_vec.shape[0]
    row_count = block_vec.shape[1]
    width_two = block_vec.shape[2]
    slots_per = pairs.shape[2]
    term_total = left_factor.shape[0]
    all_count = groups * local_blocks
    cols = width_two // pieces
    incoming = lax.dynamic_index_in_dim(pairs, owner, 1, keepdims=False)
    counts = lax.dynamic_index_in_dim(pair_count, owner, 1, keepdims=False)
    live_mask = (jnp.arange(slots_per)[None, :] < counts[:, None]).astype(jnp.float32)
    target_term = incoming[..., 1] * term_total + incoming[..., 2]
    source = jnp.arange(groups, dtype=jnp.int32)[:, None] * local_blocks + incoming[..., 0]
    key_onehot = (
        target_term[..., None] == jnp.arange(local_blocks * term_total)[None, None, :]
    ).astype(jnp.float32) * live_mask[..., None]
    ring = 4
    core = owner % 2
    here_x = owner // (2 * ring)
    here_y = (owner // 2) % ring
    offsets = jnp.arange(ring, dtype=jnp.int32)
    plane_group = (((here_x + offsets[None, :]) % ring) * ring + (here_y + offsets[:, None]) % ring) * 2
    side_group = plane_group[None] + jnp.stack([core, 1 - core])[:, None, None]
    block_ids = (side_group[..., None] * local_blocks + jnp.arange(local_blocks)).reshape(-1)
    source_onehot = (source[..., None] == block_ids[None, None, :]).astype(jnp.float32)
    weights = jnp.einsum("gqk,gqs->ks", key_onehot, source_onehot).astype(jnp.bfloat16)
    weights = weights.reshape(local_blocks * term_total, 2, ring, ring, local_blocks)

    def move(piece, dx, dy, sibling=False):
        pairs_list = []
        for b in range(groups):
            bx, by, bc = b // (2 * ring), (b // 2) % ring, b % 2
            if sibling:
                dest = b ^ 1
            else:
                dest = (((bx + dx) % ring) * ring + (by + dy) % ring) * 2 + bc
            pairs_list.append((b, dest))
        return lax.ppermute(piece, "blk", pairs_list)

    half_blocks = local_blocks // 2
    from_left = move(block_vec, 1, 0)
    from_right = move(block_vec, -1, 0)
    far = jnp.concatenate(
        [move(from_left[:half_blocks], 1, 0), move(from_right[half_blocks:], -1, 0)], axis=0
    )
    x_row = jnp.stack([block_vec, from_right, far, from_left])
    side_x = move(x_row, 0, 0, sibling=True)
    from_below = move(x_row, 0, 1)
    from_above = move(x_row, 0, -1)
    side_above = move(from_above, 0, 0, sibling=True)
    side_below = move(from_below, 0, 0, sibling=True)
    half_ring = ring // 2
    far_y = jnp.concatenate(
        [move(from_below[:half_ring], 0, 1), move(from_above[half_ring:], 0, -1)], axis=0
    )
    side_far = move(far_y, 0, 0, sibling=True)

    def pool(w, piece):
        return jnp.einsum("kab,abrn->krn", w, piece, preferred_element_type=jnp.float32)

    pooled = (
        pool(weights[:, 0, 0], x_row)
        + pool(weights[:, 0, 1], from_above)
        + pool(weights[:, 0, 2], far_y)
        + pool(weights[:, 0, 3], from_below)
        + pool(weights[:, 1, 0], side_x)
        + pool(weights[:, 1, 1], side_above)
        + pool(weights[:, 1, 2], side_far)
        + pool(weights[:, 1, 3], side_below)
    ).astype(jnp.bfloat16)
    pooled = pooled.reshape(local_blocks, term_total, row_count, width_two)
    right_done = jnp.einsum(
        "ktrn,tmn->ktrm", pooled, right_factor, preferred_element_type=jnp.float32
    ).astype(jnp.bfloat16)
    left_part = lax.dynamic_slice_in_dim(left_factor, part * row_count, row_count, axis=2)
    rates_run, pooled = lax.optimization_barrier((left_rates[None], pooled))

    def shift_sub(piece, k):
        return lax.ppermute(piece, "sub", [(j, (j + k) % pieces) for j in range(pieces)])

    trio = jnp.concatenate([shift_sub(rates_run, 1), rates_run, shift_sub(rates_run, -1)], axis=0)
    rates_run = jnp.concatenate([shift_sub(trio, 3), trio, shift_sub(trio, -3)[:2]], axis=0)
    rates_twice = jnp.concatenate([rates_run, rates_run], axis=0)
    rates_parts = lax.dynamic_slice_in_dim(rates_twice, (4 - part) % pieces, pieces, axis=0)
    rates_full = jnp.moveaxis(rates_parts, 0, 1).reshape(local_blocks, width_two)
    partial = jnp.einsum(
        "tab,ktbc->kac", left_part, right_done, preferred_element_type=jnp.float32
    ).astype(jnp.bfloat16)
    dual_cols = jnp.einsum(
        "jab,jbc->jac", left_dual, partial, preferred_element_type=jnp.float32
    ).astype(jnp.bfloat16)
    mixed = jnp.einsum("jrn,jmn->jrm", dual_cols, right_dual, preferred_element_type=jnp.float32)
    scaled = (mixed / (rates_full[:, :, None] + right_rates[:, None, :])).astype(jnp.bfloat16)
    basis_rows = jnp.einsum(
        "jrm,jkm->jrk", scaled, right_eigenvector_matrix, preferred_element_type=jnp.float32
    ).astype(jnp.bfloat16)
    basis_rows = basis_rows.reshape(local_blocks, width_two, pieces, cols)
    spread = jnp.einsum(
        "jab,jbkc->kjac", left_basis, basis_rows, preferred_element_type=jnp.float32
    ).astype(jnp.bfloat16)
    return scatter_sum(spread, "sub")


def solution(mesh):
    placed = (
        P("blk", "sub", None),
        P(),
        P(),
        P(),
        P(),
        P("blk", None, None),
        P("blk", None, None),
        P("blk", None, None),
        P("blk", None, None),
        P("blk", "sub"),
        P("blk", None),
    )
    return jax.shard_map(
        local, mesh=mesh, in_specs=placed, out_specs=P("blk", None, "sub"), check_vma=False
    )
```

```python
import jax
import jax.numpy as jnp
from jax import lax
from jax.sharding import PartitionSpec as P


def scatter_sum(chunks, axis):
    n = chunks.shape[0]
    me = lax.axis_index(axis)
    total = lax.dynamic_index_in_dim(chunks, me, 0, keepdims=False).astype(jnp.float32)
    for k in range(1, n):
        send = lax.dynamic_index_in_dim(chunks, (me + k) % n, 0, keepdims=False)
        got = lax.ppermute(send, axis, [(j, (j + k) % n) for j in range(n)])
        total = total + got.astype(jnp.float32)
    return total


def local(
    block_vec,
    left_factor,
    right_factor,
    pairs,
    pair_count,
    left_basis,
    left_dual,
    right_eigenvector_matrix,
    right_dual,
    left_rates,
    right_rates,
):
    owner = lax.axis_index("blk")
    part = lax.axis_index("sub")
    groups = lax.axis_size("blk")
    pieces = lax.axis_size("sub")
    local_blocks = block_vec.shape[0]
    row_count = block_vec.shape[1]
    width_two = block_vec.shape[2]
    slots_per = pairs.shape[2]
    term_total = left_factor.shape[0]
    all_count = groups * local_blocks
    cols = width_two // pieces
    incoming = lax.dynamic_index_in_dim(pairs, owner, 1, keepdims=False)
    counts = lax.dynamic_index_in_dim(pair_count, owner, 1, keepdims=False)
    live_mask = (jnp.arange(slots_per)[None, :] < counts[:, None]).astype(jnp.float32)
    target_term = incoming[..., 1] * term_total + incoming[..., 2]
    source = jnp.arange(groups, dtype=jnp.int32)[:, None] * local_blocks + incoming[..., 0]
    key_onehot = (
        target_term[..., None] == jnp.arange(local_blocks * term_total)[None, None, :]
    ).astype(jnp.float32) * live_mask[..., None]
    ring = 4
    core = owner % 2
    here_x = owner // (2 * ring)
    here_y = (owner // 2) % ring
    offsets = jnp.arange(ring, dtype=jnp.int32)
    plane_group = (((here_x + offsets[None, :]) % ring) * ring + (here_y + offsets[:, None]) % ring) * 2
    side_group = plane_group[None] + jnp.stack([core, 1 - core])[:, None, None]
    block_ids = (side_group[..., None] * local_blocks + jnp.arange(local_blocks)).reshape(-1)
    source_onehot = (source[..., None] == block_ids[None, None, :]).astype(jnp.float32)
    weights = jnp.einsum("gqk,gqs->ks", key_onehot, source_onehot).astype(jnp.bfloat16)
    weights = weights.reshape(local_blocks * term_total, 2, ring, ring, local_blocks)

    def move(piece, dx, dy, sibling=False):
        pairs_list = []
        for b in range(groups):
            bx, by, bc = b // (2 * ring), (b // 2) % ring, b % 2
            if sibling:
                dest = b ^ 1
            else:
                dest = (((bx + dx) % ring) * ring + (by + dy) % ring) * 2 + bc
            pairs_list.append((b, dest))
        return lax.ppermute(piece, "blk", pairs_list)

    half_blocks = local_blocks // 2
    from_left = move(block_vec, 1, 0)
    from_right = move(block_vec, -1, 0)
    far = jnp.concatenate(
        [move(from_left[:half_blocks], 1, 0), move(from_right[half_blocks:], -1, 0)], axis=0
    )
    x_row = jnp.stack([block_vec, from_right, far, from_left])
    rates_seed, x_row = lax.optimization_barrier((left_rates[None], x_row))
    side_x = move(x_row, 0, 0, sibling=True)
    from_below = move(x_row, 0, 1)
    from_above = move(x_row, 0, -1)
    side_above = move(from_above, 0, 0, sibling=True)
    side_below = move(from_below, 0, 0, sibling=True)
    half_ring = ring // 2
    far_y = jnp.concatenate(
        [move(from_below[:half_ring], 0, 1), move(from_above[half_ring:], 0, -1)], axis=0
    )
    side_far = move(far_y, 0, 0, sibling=True)

    def pool(w, piece):
        return jnp.einsum("kab,abrn->krn", w, piece, preferred_element_type=jnp.float32)

    pooled = (
        pool(weights[:, 0, 0], x_row)
        + pool(weights[:, 0, 1], from_above)
        + pool(weights[:, 0, 2], far_y)
        + pool(weights[:, 0, 3], from_below)
        + pool(weights[:, 1, 0], side_x)
        + pool(weights[:, 1, 1], side_above)
        + pool(weights[:, 1, 2], side_far)
        + pool(weights[:, 1, 3], side_below)
    ).astype(jnp.bfloat16)
    pooled = pooled.reshape(local_blocks, term_total, row_count, width_two)
    right_done = jnp.einsum(
        "ktrn,tmn->ktrm", pooled, right_factor, preferred_element_type=jnp.float32
    ).astype(jnp.bfloat16)
    left_part = lax.dynamic_slice_in_dim(left_factor, part * row_count, row_count, axis=2)
    rates_run = rates_seed

    def shift_sub(piece, k):
        return lax.ppermute(piece, "sub", [(j, (j + k) % pieces) for j in range(pieces)])

    trio = jnp.concatenate([shift_sub(rates_run, 1), rates_run, shift_sub(rates_run, -1)], axis=0)
    rates_run = jnp.concatenate([shift_sub(trio, 3), trio, shift_sub(trio, -3)[:2]], axis=0)
    rates_twice = jnp.concatenate([rates_run, rates_run], axis=0)
    rates_parts = lax.dynamic_slice_in_dim(rates_twice, (4 - part) % pieces, pieces, axis=0)
    rates_full = jnp.moveaxis(rates_parts, 0, 1).reshape(local_blocks, width_two)
    partial = jnp.einsum(
        "tab,ktbc->kac", left_part, right_done, preferred_element_type=jnp.float32
    ).astype(jnp.bfloat16)
    dual_cols = jnp.einsum(
        "jab,jbc->jac", left_dual, partial, preferred_element_type=jnp.float32
    ).astype(jnp.bfloat16)
    mixed = jnp.einsum("jrn,jmn->jrm", dual_cols, right_dual, preferred_element_type=jnp.float32)
    scaled = (mixed / (rates_full[:, :, None] + right_rates[:, None, :])).astype(jnp.bfloat16)
    basis_rows = jnp.einsum(
        "jrm,jkm->jrk", scaled, right_eigenvector_matrix, preferred_element_type=jnp.float32
    ).astype(jnp.bfloat16)
    basis_rows = basis_rows.reshape(local_blocks, width_two, pieces, cols)
    spread = jnp.einsum(
        "jab,jbkc->kjac", left_basis, basis_rows, preferred_element_type=jnp.float32
    ).astype(jnp.bfloat16)
    return scatter_sum(spread, "sub")


def solution(mesh):
    placed = (
        P("blk", "sub", None),
        P(),
        P(),
        P(),
        P(),
        P("blk", None, None),
        P("blk", None, None),
        P("blk", None, None),
        P("blk", None, None),
        P("blk", "sub"),
        P("blk", None),
    )
    return jax.shard_map(
        local, mesh=mesh, in_specs=placed, out_specs=P("blk", None, "sub"), check_vma=False
    )
```

```python
import jax
import jax.numpy as jnp
from jax import lax
from jax.sharding import PartitionSpec as P


def scatter_sum(chunks, axis):
    n = chunks.shape[0]
    me = lax.axis_index(axis)
    total = lax.dynamic_index_in_dim(chunks, me, 0, keepdims=False).astype(jnp.float32)
    for k in range(1, n):
        send = lax.dynamic_index_in_dim(chunks, (me + k) % n, 0, keepdims=False)
        got = lax.ppermute(send, axis, [(j, (j + k) % n) for j in range(n)])
        total = total + got.astype(jnp.float32)
    return total


def local(
    block_vec,
    left_factor,
    right_factor,
    pairs,
    pair_count,
    left_basis,
    left_dual,
    right_eigenvector_matrix,
    right_dual,
    left_rates,
    right_rates,
):
    owner = lax.axis_index("blk")
    part = lax.axis_index("sub")
    groups = lax.axis_size("blk")
    pieces = lax.axis_size("sub")
    local_blocks = block_vec.shape[0]
    row_count = block_vec.shape[1]
    width_two = block_vec.shape[2]
    slots_per = pairs.shape[2]
    term_total = left_factor.shape[0]
    all_count = groups * local_blocks
    cols = width_two // pieces
    incoming = lax.dynamic_index_in_dim(pairs, owner, 1, keepdims=False)
    counts = lax.dynamic_index_in_dim(pair_count, owner, 1, keepdims=False)
    live_mask = (jnp.arange(slots_per)[None, :] < counts[:, None]).astype(jnp.float32)
    target_term = incoming[..., 1] * term_total + incoming[..., 2]
    source = jnp.arange(groups, dtype=jnp.int32)[:, None] * local_blocks + incoming[..., 0]
    key_onehot = (
        target_term[..., None] == jnp.arange(local_blocks * term_total)[None, None, :]
    ).astype(jnp.float32) * live_mask[..., None]
    ring = 4
    core = owner % 2
    here_x = owner // (2 * ring)
    here_y = (owner // 2) % ring
    offsets = jnp.arange(ring, dtype=jnp.int32)
    plane_group = (((here_x + offsets[None, :]) % ring) * ring + (here_y + offsets[:, None]) % ring) * 2
    side_group = plane_group[None] + jnp.stack([core, 1 - core])[:, None, None]
    block_ids = (side_group[..., None] * local_blocks + jnp.arange(local_blocks)).reshape(-1)
    source_onehot = (source[..., None] == block_ids[None, None, :]).astype(jnp.float32)
    weights = jnp.einsum("gqk,gqs->ks", key_onehot, source_onehot).astype(jnp.bfloat16)
    weights = weights.reshape(local_blocks * term_total, 2, ring, ring, local_blocks)

    def move(piece, dx, dy, sibling=False):
        pairs_list = []
        for b in range(groups):
            bx, by, bc = b // (2 * ring), (b // 2) % ring, b % 2
            if sibling:
                dest = b ^ 1
            else:
                dest = (((bx + dx) % ring) * ring + (by + dy) % ring) * 2 + bc
            pairs_list.append((b, dest))
        return lax.ppermute(piece, "blk", pairs_list)

    half_blocks = local_blocks // 2
    from_left = move(block_vec, 1, 0)
    from_right = move(block_vec, -1, 0)
    far = jnp.concatenate(
        [move(from_left[:half_blocks], 1, 0), move(from_right[half_blocks:], -1, 0)], axis=0
    )
    x_row = jnp.stack([block_vec, from_right, far, from_left])
    side_x = move(x_row, 0, 0, sibling=True)
    from_below = move(x_row, 0, 1)
    from_above = move(x_row, 0, -1)
    side_above = move(from_above, 0, 0, sibling=True)
    side_below = move(from_below, 0, 0, sibling=True)
    half_ring = ring // 2
    far_y = jnp.concatenate(
        [move(from_below[:half_ring], 0, 1), move(from_above[half_ring:], 0, -1)], axis=0
    )
    side_far = move(far_y, 0, 0, sibling=True)

    def pool(w, piece):
        return jnp.einsum("kab,abrn->krn", w, piece, preferred_element_type=jnp.float32)

    pooled = (
        pool(weights[:, 0, 0], x_row)
        + pool(weights[:, 0, 1], from_above)
        + pool(weights[:, 0, 2], far_y)
        + pool(weights[:, 0, 3], from_below)
        + pool(weights[:, 1, 0], side_x)
        + pool(weights[:, 1, 1], side_above)
        + pool(weights[:, 1, 2], side_far)
        + pool(weights[:, 1, 3], side_below)
    ).astype(jnp.bfloat16)
    pooled = pooled.reshape(local_blocks, term_total, row_count, width_two)
    right_done = jnp.einsum(
        "ktrn,tmn->ktrm", pooled, right_factor, preferred_element_type=jnp.float32
    ).astype(jnp.bfloat16)
    left_part = lax.dynamic_slice_in_dim(left_factor, part * row_count, row_count, axis=2)
    rates_run = left_rates[None]

    def shift_sub(piece, k):
        return lax.ppermute(piece, "sub", [(j, (j + k) % pieces) for j in range(pieces)])

    trio = jnp.concatenate([shift_sub(rates_run, 1), rates_run, shift_sub(rates_run, -1)], axis=0)
    rates_run = jnp.concatenate([shift_sub(trio, 3), trio, shift_sub(trio, -3)[:2]], axis=0)
    rates_twice = jnp.concatenate([rates_run, rates_run], axis=0)
    rates_parts = lax.dynamic_slice_in_dim(rates_twice, (4 - part) % pieces, pieces, axis=0)
    rates_full = jnp.moveaxis(rates_parts, 0, 1).reshape(local_blocks, width_two)
    partial = jnp.einsum(
        "tab,ktbc->kac", left_part, right_done, preferred_element_type=jnp.float32
    ).astype(jnp.bfloat16)
    dual_cols = jnp.einsum(
        "jab,jbc->jac", left_dual, partial, preferred_element_type=jnp.float32
    ).astype(jnp.bfloat16)
    mixed = jnp.einsum("jrn,jmn->jrm", dual_cols, right_dual, preferred_element_type=jnp.float32)
    scaled = (mixed / (rates_full[:, :, None] + right_rates[:, None, :])).astype(jnp.bfloat16)
    basis_rows = jnp.einsum(
        "jrm,jkm->jrk", scaled, right_eigenvector_matrix, preferred_element_type=jnp.float32
    ).astype(jnp.bfloat16)
    basis_rows = basis_rows.reshape(local_blocks, width_two, pieces, cols)
    spread = jnp.einsum(
        "jab,jbkc->kjac", left_basis, basis_rows, preferred_element_type=jnp.float32
    ).astype(jnp.bfloat16)
    return scatter_sum(spread, "sub")


def solution(mesh):
    placed = (
        P("blk", "sub", None),
        P(),
        P(),
        P(),
        P(),
        P("blk", None, None),
        P("blk", None, None),
        P("blk", None, None),
        P("blk", None, None),
        P("blk", "sub"),
        P("blk", None),
    )
    return jax.shard_map(
        local, mesh=mesh, in_specs=placed, out_specs=P("blk", None, "sub"), check_vma=False
    )
```

```python
import jax
import jax.numpy as jnp
from jax import lax
from jax.sharding import PartitionSpec as P


def scatter_sum(chunks, axis):
    n = chunks.shape[0]
    me = lax.axis_index(axis)
    total = lax.dynamic_index_in_dim(chunks, me, 0, keepdims=False).astype(jnp.float32)
    for k in range(1, n):
        send = lax.dynamic_index_in_dim(chunks, (me + k) % n, 0, keepdims=False)
        got = lax.ppermute(send, axis, [(j, (j + k) % n) for j in range(n)])
        total = total + got.astype(jnp.float32)
    return total


def local(
    block_vec,
    left_factor,
    right_factor,
    pairs,
    pair_count,
    left_basis,
    left_dual,
    right_eigenvector_matrix,
    right_dual,
    left_rates,
    right_rates,
):
    owner = lax.axis_index("blk")
    part = lax.axis_index("sub")
    groups = lax.axis_size("blk")
    pieces = lax.axis_size("sub")
    local_blocks = block_vec.shape[0]
    row_count = block_vec.shape[1]
    width_two = block_vec.shape[2]
    slots_per = pairs.shape[2]
    term_total = left_factor.shape[0]
    all_count = groups * local_blocks
    cols = width_two // pieces
    incoming = lax.dynamic_index_in_dim(pairs, owner, 1, keepdims=False)
    counts = lax.dynamic_index_in_dim(pair_count, owner, 1, keepdims=False)
    live_mask = (jnp.arange(slots_per)[None, :] < counts[:, None]).astype(jnp.float32)
    target_term = incoming[..., 1] * term_total + incoming[..., 2]
    source = jnp.arange(groups, dtype=jnp.int32)[:, None] * local_blocks + incoming[..., 0]
    key_onehot = (
        target_term[..., None] == jnp.arange(local_blocks * term_total)[None, None, :]
    ).astype(jnp.float32) * live_mask[..., None]
    ring = 4
    core = owner % 2
    here_x = owner // (2 * ring)
    here_y = (owner // 2) % ring
    offsets = jnp.arange(ring, dtype=jnp.int32)
    plane_group = (((here_x + offsets[None, :]) % ring) * ring + (here_y + offsets[:, None]) % ring) * 2
    side_group = plane_group[None] + jnp.stack([core, 1 - core])[:, None, None]
    block_ids = (side_group[..., None] * local_blocks + jnp.arange(local_blocks)).reshape(-1)
    source_onehot = (source[..., None] == block_ids[None, None, :]).astype(jnp.float32)
    weights = jnp.einsum("gqk,gqs->ks", key_onehot, source_onehot).astype(jnp.bfloat16)
    weights = weights.reshape(local_blocks * term_total, 2, ring, ring, local_blocks)

    def move(piece, dx, dy, sibling=False):
        pairs_list = []
        for b in range(groups):
            bx, by, bc = b // (2 * ring), (b // 2) % ring, b % 2
            if sibling:
                dest = b ^ 1
            else:
                dest = (((bx + dx) % ring) * ring + (by + dy) % ring) * 2 + bc
            pairs_list.append((b, dest))
        return lax.ppermute(piece, "blk", pairs_list)

    half_blocks = local_blocks // 2
    from_left = move(block_vec, 1, 0)
    from_right = move(block_vec, -1, 0)
    far = jnp.concatenate(
        [move(from_left[:half_blocks], 1, 0), move(from_right[half_blocks:], -1, 0)], axis=0
    )
    x_row = jnp.stack([block_vec, from_right, far, from_left])
    side_x = move(x_row, 0, 0, sibling=True)
    from_below = move(x_row, 0, 1)
    from_above = move(x_row, 0, -1)
    side_above = move(from_above, 0, 0, sibling=True)
    side_below = move(from_below, 0, 0, sibling=True)
    half_ring = ring // 2
    far_y = jnp.concatenate(
        [move(from_below[:half_ring], 0, 1), move(from_above[half_ring:], 0, -1)], axis=0
    )
    side_far = move(far_y, 0, 0, sibling=True)

    def pool(w, piece):
        return jnp.einsum("kab,abrn->krn", w, piece, preferred_element_type=jnp.float32)

    pooled = (
        pool(weights[:, 0, 0], x_row)
        + pool(weights[:, 0, 1], from_above)
        + pool(weights[:, 0, 2], far_y)
        + pool(weights[:, 0, 3], from_below)
        + pool(weights[:, 1, 0], side_x)
        + pool(weights[:, 1, 1], side_above)
        + pool(weights[:, 1, 2], side_far)
        + pool(weights[:, 1, 3], side_below)
    ).astype(jnp.bfloat16)
    pooled = pooled.reshape(local_blocks, term_total, row_count, width_two)
    right_done = jnp.einsum(
        "ktrn,tmn->ktrm", pooled, right_factor, preferred_element_type=jnp.float32
    ).astype(jnp.bfloat16)
    left_part = lax.dynamic_slice_in_dim(left_factor, part * row_count, row_count, axis=2)
    left_flat = jnp.transpose(left_part, (1, 0, 2)).reshape(width_two, term_total * row_count)
    done_flat = right_done.reshape(local_blocks, term_total * row_count, width_two)
    left_flat, done_flat = lax.optimization_barrier((left_flat, done_flat))
    partial = jnp.einsum(
        "ak,jkc->jac", left_flat, done_flat, preferred_element_type=jnp.float32
    ).astype(jnp.bfloat16)
    dual_cols = jnp.einsum(
        "jab,jbc->jac", left_dual, partial, preferred_element_type=jnp.float32
    ).astype(jnp.bfloat16)
    dual_cols = dual_cols.reshape(local_blocks, pieces, row_count, width_two)
    mixed_parts = jnp.einsum(
        "jsrn,jmn->sjrm", dual_cols, right_dual, preferred_element_type=jnp.float32
    ).astype(jnp.bfloat16)
    mixed = scatter_sum(mixed_parts, "sub")
    scaled = (mixed / (left_rates[:, :, None] + right_rates[:, None, :])).astype(jnp.bfloat16)
    basis_rows = jnp.einsum(
        "jrm,jkm->jrk", scaled, right_eigenvector_matrix, preferred_element_type=jnp.float32
    ).astype(jnp.bfloat16)
    basis_cols = lax.all_to_all(basis_rows, "sub", split_axis=2, concat_axis=1, tiled=True)
    return jnp.einsum("jab,jbc->jac", left_basis, basis_cols, preferred_element_type=jnp.float32)


def solution(mesh):
    placed = (
        P("blk", "sub", None),
        P(),
        P(),
        P(),
        P(),
        P("blk", None, None),
        P("blk", None, None),
        P("blk", None, None),
        P("blk", None, None),
        P("blk", "sub"),
        P("blk", None),
    )
    return jax.shard_map(
        local, mesh=mesh, in_specs=placed, out_specs=P("blk", None, "sub"), check_vma=False
    )
```

```python
import jax
import jax.numpy as jnp
from jax import lax
from jax.sharding import PartitionSpec as P


def scatter_sum(chunks, axis):
    n = chunks.shape[0]
    me = lax.axis_index(axis)
    total = lax.dynamic_index_in_dim(chunks, me, 0, keepdims=False).astype(jnp.float32)
    for k in range(1, n):
        send = lax.dynamic_index_in_dim(chunks, (me + k) % n, 0, keepdims=False)
        got = lax.ppermute(send, axis, [(j, (j + k) % n) for j in range(n)])
        total = total + got.astype(jnp.float32)
    return total


def local(
    block_vec,
    left_factor,
    right_factor,
    pairs,
    pair_count,
    left_basis,
    left_dual,
    right_eigenvector_matrix,
    right_dual,
    left_rates,
    right_rates,
):
    owner = lax.axis_index("blk")
    part = lax.axis_index("sub")
    groups = lax.axis_size("blk")
    pieces = lax.axis_size("sub")
    local_blocks = block_vec.shape[0]
    row_count = block_vec.shape[1]
    width_two = block_vec.shape[2]
    slots_per = pairs.shape[2]
    term_total = left_factor.shape[0]
    all_count = groups * local_blocks
    cols = width_two // pieces
    incoming = lax.dynamic_index_in_dim(pairs, owner, 1, keepdims=False)
    counts = lax.dynamic_index_in_dim(pair_count, owner, 1, keepdims=False)
    live_mask = (jnp.arange(slots_per)[None, :] < counts[:, None]).astype(jnp.float32)
    target_term = incoming[..., 1] * term_total + incoming[..., 2]
    source = jnp.arange(groups, dtype=jnp.int32)[:, None] * local_blocks + incoming[..., 0]
    key_onehot = (
        target_term[..., None] == jnp.arange(local_blocks * term_total)[None, None, :]
    ).astype(jnp.float32) * live_mask[..., None]
    ring = 4
    core = owner % 2
    here_x = owner // (2 * ring)
    here_y = (owner // 2) % ring
    offsets = jnp.arange(ring, dtype=jnp.int32)
    plane_group = (((here_x + offsets[None, :]) % ring) * ring + (here_y + offsets[:, None]) % ring) * 2
    side_group = plane_group[None] + jnp.stack([core, 1 - core])[:, None, None]
    block_ids = (side_group[..., None] * local_blocks + jnp.arange(local_blocks)).reshape(-1)
    source_onehot = (source[..., None] == block_ids[None, None, :]).astype(jnp.float32)
    weights = jnp.einsum("gqk,gqs->ks", key_onehot, source_onehot).astype(jnp.bfloat16)
    weights = weights.reshape(local_blocks * term_total, 2, ring, ring, local_blocks)

    def move(piece, dx, dy, sibling=False):
        pairs_list = []
        for b in range(groups):
            bx, by, bc = b // (2 * ring), (b // 2) % ring, b % 2
            if sibling:
                dest = b ^ 1
            else:
                dest = (((bx + dx) % ring) * ring + (by + dy) % ring) * 2 + bc
            pairs_list.append((b, dest))
        return lax.ppermute(piece, "blk", pairs_list)

    half_blocks = local_blocks // 2
    from_left = move(block_vec, 1, 0)
    from_right = move(block_vec, -1, 0)
    far = jnp.concatenate(
        [move(from_left[:half_blocks], 1, 0), move(from_right[half_blocks:], -1, 0)], axis=0
    )
    x_row = jnp.stack([block_vec, from_right, far, from_left])
    side_x = move(x_row, 0, 0, sibling=True)
    from_below = move(x_row, 0, 1)
    from_above = move(x_row, 0, -1)
    side_above = move(from_above, 0, 0, sibling=True)
    side_below = move(from_below, 0, 0, sibling=True)
    half_ring = ring // 2
    far_y = jnp.concatenate(
        [move(from_below[:half_ring], 0, 1), move(from_above[half_ring:], 0, -1)], axis=0
    )
    side_far = move(far_y, 0, 0, sibling=True)

    def pool(w, piece):
        return jnp.einsum("kab,abrn->krn", w, piece, preferred_element_type=jnp.float32)

    pooled = (
        pool(weights[:, 0, 0], x_row)
        + pool(weights[:, 0, 1], from_above)
        + pool(weights[:, 0, 2], far_y)
        + pool(weights[:, 0, 3], from_below)
        + pool(weights[:, 1, 0], side_x)
        + pool(weights[:, 1, 1], side_above)
        + pool(weights[:, 1, 2], side_far)
        + pool(weights[:, 1, 3], side_below)
    ).astype(jnp.bfloat16)
    pooled = pooled.reshape(local_blocks, term_total, row_count, width_two)
    right_done = jnp.einsum(
        "ktrn,tmn->ktrm", pooled, right_factor, preferred_element_type=jnp.float32
    ).astype(jnp.bfloat16)
    left_part = lax.dynamic_slice_in_dim(left_factor, part * row_count, row_count, axis=2)
    rates_run, pooled = lax.optimization_barrier((left_rates[None], pooled))
    rates_parts = lax.all_to_all(
        jnp.broadcast_to(rates_run, (pieces,) + left_rates.shape), "sub", 0, 0, tiled=True
    )
    rates_full = jnp.moveaxis(rates_parts, 0, 1).reshape(local_blocks, width_two)
    partial = jnp.einsum(
        "tab,ktbc->kac", left_part, right_done, preferred_element_type=jnp.float32
    ).astype(jnp.bfloat16)
    dual_cols = jnp.einsum(
        "jab,jbc->jac", left_dual, partial, preferred_element_type=jnp.float32
    ).astype(jnp.bfloat16)
    mixed = jnp.einsum("jrn,jmn->jrm", dual_cols, right_dual, preferred_element_type=jnp.float32)
    scaled = (mixed / (rates_full[:, :, None] + right_rates[:, None, :])).astype(jnp.bfloat16)
    basis_rows = jnp.einsum(
        "jrm,jkm->jrk", scaled, right_eigenvector_matrix, preferred_element_type=jnp.float32
    ).astype(jnp.bfloat16)
    basis_rows = basis_rows.reshape(local_blocks, width_two, pieces, cols)
    spread = jnp.einsum(
        "jab,jbkc->kjac", left_basis, basis_rows, preferred_element_type=jnp.float32
    ).astype(jnp.bfloat16)
    return scatter_sum(spread, "sub")


def solution(mesh):
    placed = (
        P("blk", "sub", None),
        P(),
        P(),
        P(),
        P(),
        P("blk", None, None),
        P("blk", None, None),
        P("blk", None, None),
        P("blk", None, None),
        P("blk", "sub"),
        P("blk", None),
    )
    return jax.shard_map(
        local, mesh=mesh, in_specs=placed, out_specs=P("blk", None, "sub"), check_vma=False
    )
```

```python
import jax
import jax.numpy as jnp
from jax import lax
from jax.sharding import PartitionSpec as P


def scatter_sum(chunks, axis):
    n = chunks.shape[0]
    me = lax.axis_index(axis)
    total = lax.dynamic_index_in_dim(chunks, me, 0, keepdims=False).astype(jnp.float32)
    for k in range(1, n):
        send = lax.dynamic_index_in_dim(chunks, (me + k) % n, 0, keepdims=False)
        got = lax.ppermute(send, axis, [(j, (j + k) % n) for j in range(n)])
        total = total + got.astype(jnp.float32)
    return total


def local(
    block_vec,
    left_factor,
    right_factor,
    pairs,
    pair_count,
    left_basis,
    left_dual,
    right_eigenvector_matrix,
    right_dual,
    left_rates,
    right_rates,
):
    owner = lax.axis_index("blk")
    part = lax.axis_index("sub")
    groups = lax.axis_size("blk")
    pieces = lax.axis_size("sub")
    local_blocks = block_vec.shape[0]
    row_count = block_vec.shape[1]
    width_two = block_vec.shape[2]
    slots_per = pairs.shape[2]
    term_total = left_factor.shape[0]
    all_count = groups * local_blocks
    cols = width_two // pieces
    incoming = lax.dynamic_index_in_dim(pairs, owner, 1, keepdims=False)
    counts = lax.dynamic_index_in_dim(pair_count, owner, 1, keepdims=False)
    live_mask = (jnp.arange(slots_per)[None, :] < counts[:, None]).astype(jnp.float32)
    target_term = incoming[..., 1] * term_total + incoming[..., 2]
    source = jnp.arange(groups, dtype=jnp.int32)[:, None] * local_blocks + incoming[..., 0]
    key_onehot = (
        target_term[..., None] == jnp.arange(local_blocks * term_total)[None, None, :]
    ).astype(jnp.float32) * live_mask[..., None]
    ring = 4
    core = owner % 2
    here_x = owner // (2 * ring)
    here_y = (owner // 2) % ring
    offsets = jnp.arange(ring, dtype=jnp.int32)
    plane_group = (((here_x + offsets[None, :]) % ring) * ring + (here_y + offsets[:, None]) % ring) * 2
    side_group = plane_group[None] + jnp.stack([core, 1 - core])[:, None, None]
    block_ids = (side_group[..., None] * local_blocks + jnp.arange(local_blocks)).reshape(-1)
    source_onehot = (source[..., None] == block_ids[None, None, :]).astype(jnp.float32)
    weights = jnp.einsum("gqk,gqs->ks", key_onehot, source_onehot).astype(jnp.bfloat16)
    weights = weights.reshape(local_blocks * term_total, 2, ring, ring, local_blocks)

    def move(piece, dx, dy, sibling=False):
        pairs_list = []
        for b in range(groups):
            bx, by, bc = b // (2 * ring), (b // 2) % ring, b % 2
            if sibling:
                dest = b ^ 1
            else:
                dest = (((bx + dx) % ring) * ring + (by + dy) % ring) * 2 + bc
            pairs_list.append((b, dest))
        return lax.ppermute(piece, "blk", pairs_list)

    half_blocks = local_blocks // 2
    from_left = move(block_vec, 1, 0)
    from_right = move(block_vec, -1, 0)
    far = jnp.concatenate(
        [move(from_left[:half_blocks], 1, 0), move(from_right[half_blocks:], -1, 0)], axis=0
    )
    x_row = jnp.stack([block_vec, from_right, far, from_left])
    side_x = move(x_row, 0, 0, sibling=True)
    from_below = move(x_row, 0, 1)
    from_above = move(x_row, 0, -1)
    side_above = move(from_above, 0, 0, sibling=True)
    side_below = move(from_below, 0, 0, sibling=True)
    half_ring = ring // 2
    far_y = jnp.concatenate(
        [move(from_below[:half_ring], 0, 1), move(from_above[half_ring:], 0, -1)], axis=0
    )
    side_far = move(far_y, 0, 0, sibling=True)

    def pool(w, piece):
        return jnp.einsum("kab,abrn->krn", w, piece, preferred_element_type=jnp.float32)

    pooled = (
        pool(weights[:, 0, 0], x_row)
        + pool(weights[:, 0, 1], from_above)
        + pool(weights[:, 0, 2], far_y)
        + pool(weights[:, 0, 3], from_below)
        + pool(weights[:, 1, 0], side_x)
        + pool(weights[:, 1, 1], side_above)
        + pool(weights[:, 1, 2], side_far)
        + pool(weights[:, 1, 3], side_below)
    ).astype(jnp.bfloat16)
    pooled = pooled.reshape(local_blocks, term_total, row_count, width_two)
    right_done = jnp.einsum(
        "ktrn,tmn->ktrm", pooled, right_factor, preferred_element_type=jnp.float32
    ).astype(jnp.bfloat16)
    left_part = lax.dynamic_slice_in_dim(left_factor, part * row_count, row_count, axis=2)
    rates_run = left_rates[None]
    rates_parts = lax.all_to_all(
        jnp.broadcast_to(rates_run, (pieces,) + left_rates.shape), "sub", 0, 0, tiled=True
    )
    rates_full = jnp.moveaxis(rates_parts, 0, 1).reshape(local_blocks, width_two)
    partial = jnp.einsum(
        "tab,ktbc->kac", left_part, right_done, preferred_element_type=jnp.float32
    ).astype(jnp.bfloat16)
    dual_cols = jnp.einsum(
        "jab,jbc->jac", left_dual, partial, preferred_element_type=jnp.float32
    ).astype(jnp.bfloat16)
    mixed = jnp.einsum("jrn,jmn->jrm", dual_cols, right_dual, preferred_element_type=jnp.float32)
    scaled = (mixed / (rates_full[:, :, None] + right_rates[:, None, :])).astype(jnp.bfloat16)
    basis_rows = jnp.einsum(
        "jrm,jkm->jrk", scaled, right_eigenvector_matrix, preferred_element_type=jnp.float32
    ).astype(jnp.bfloat16)
    basis_rows = basis_rows.reshape(local_blocks, width_two, pieces, cols)
    spread = jnp.einsum(
        "jab,jbkc->kjac", left_basis, basis_rows, preferred_element_type=jnp.float32
    ).astype(jnp.bfloat16)
    return scatter_sum(spread, "sub")


def solution(mesh):
    placed = (
        P("blk", "sub", None),
        P(),
        P(),
        P(),
        P(),
        P("blk", None, None),
        P("blk", None, None),
        P("blk", None, None),
        P("blk", None, None),
        P("blk", "sub"),
        P("blk", None),
    )
    return jax.shard_map(
        local, mesh=mesh, in_specs=placed, out_specs=P("blk", None, "sub"), check_vma=False
    )
```

```python
import jax
import jax.numpy as jnp
from jax import lax
from jax.sharding import PartitionSpec as P


def scatter_sum(chunks, axis):
    n = chunks.shape[0]
    me = lax.axis_index(axis)
    total = lax.dynamic_index_in_dim(chunks, me, 0, keepdims=False).astype(jnp.float32)
    for k in range(1, n):
        send = lax.dynamic_index_in_dim(chunks, (me + k) % n, 0, keepdims=False)
        got = lax.ppermute(send, axis, [(j, (j + k) % n) for j in range(n)])
        total = total + got.astype(jnp.float32)
    return total


def local(
    block_vec,
    left_factor,
    right_factor,
    pairs,
    pair_count,
    left_basis,
    left_dual,
    right_eigenvector_matrix,
    right_dual,
    left_rates,
    right_rates,
):
    owner = lax.axis_index("blk")
    part = lax.axis_index("sub")
    groups = lax.axis_size("blk")
    pieces = lax.axis_size("sub")
    local_blocks = block_vec.shape[0]
    row_count = block_vec.shape[1]
    width_two = block_vec.shape[2]
    slots_per = pairs.shape[2]
    term_total = left_factor.shape[0]
    all_count = groups * local_blocks
    cols = width_two // pieces
    incoming = lax.dynamic_index_in_dim(pairs, owner, 1, keepdims=False)
    counts = lax.dynamic_index_in_dim(pair_count, owner, 1, keepdims=False)
    live_mask = (jnp.arange(slots_per)[None, :] < counts[:, None]).astype(jnp.float32)
    target_term = incoming[..., 1] * term_total + incoming[..., 2]
    source = jnp.arange(groups, dtype=jnp.int32)[:, None] * local_blocks + incoming[..., 0]
    key_onehot = (
        target_term[..., None] == jnp.arange(local_blocks * term_total)[None, None, :]
    ).astype(jnp.float32) * live_mask[..., None]
    ring = 4
    core = owner % 2
    here_x = owner // (2 * ring)
    here_y = (owner // 2) % ring
    offsets = jnp.arange(ring, dtype=jnp.int32)
    plane_group = (((here_x + offsets[None, :]) % ring) * ring + (here_y + offsets[:, None]) % ring) * 2
    side_group = plane_group[None] + jnp.stack([core, 1 - core])[:, None, None]
    block_ids = (side_group[..., None] * local_blocks + jnp.arange(local_blocks)).reshape(-1)
    source_onehot = (source[..., None] == block_ids[None, None, :]).astype(jnp.float32)
    weights = jnp.einsum("gqk,gqs->ks", key_onehot, source_onehot).astype(jnp.bfloat16)
    weights = weights.reshape(local_blocks * term_total, 2, ring, ring, local_blocks)

    def move(piece, dx, dy, sibling=False):
        pairs_list = []
        for b in range(groups):
            bx, by, bc = b // (2 * ring), (b // 2) % ring, b % 2
            if sibling:
                dest = b ^ 1
            else:
                dest = (((bx + dx) % ring) * ring + (by + dy) % ring) * 2 + bc
            pairs_list.append((b, dest))
        return lax.ppermute(piece, "blk", pairs_list)

    half_blocks = local_blocks // 2
    from_left = move(block_vec, 1, 0)
    from_right = move(block_vec, -1, 0)
    far = jnp.concatenate(
        [move(from_left[:half_blocks], 1, 0), move(from_right[half_blocks:], -1, 0)], axis=0
    )
    x_row = jnp.stack([block_vec, from_right, far, from_left])
    rates_seed, x_row = lax.optimization_barrier((left_rates[None], x_row))
    side_x = move(x_row, 0, 0, sibling=True)
    from_below = move(x_row, 0, 1)
    from_above = move(x_row, 0, -1)
    side_above = move(from_above, 0, 0, sibling=True)
    side_below = move(from_below, 0, 0, sibling=True)
    half_ring = ring // 2
    far_y = jnp.concatenate(
        [move(from_below[:half_ring], 0, 1), move(from_above[half_ring:], 0, -1)], axis=0
    )
    side_far = move(far_y, 0, 0, sibling=True)

    def pool(w, piece):
        return jnp.einsum("kab,abrn->krn", w, piece, preferred_element_type=jnp.float32)

    pooled = (
        pool(weights[:, 0, 0], x_row)
        + pool(weights[:, 0, 1], from_above)
        + pool(weights[:, 0, 2], far_y)
        + pool(weights[:, 0, 3], from_below)
        + pool(weights[:, 1, 0], side_x)
        + pool(weights[:, 1, 1], side_above)
        + pool(weights[:, 1, 2], side_far)
        + pool(weights[:, 1, 3], side_below)
    ).astype(jnp.bfloat16)
    pooled = pooled.reshape(local_blocks, term_total, row_count, width_two)
    right_done = jnp.einsum(
        "ktrn,tmn->ktrm", pooled, right_factor, preferred_element_type=jnp.float32
    ).astype(jnp.bfloat16)
    left_part = lax.dynamic_slice_in_dim(left_factor, part * row_count, row_count, axis=2)
    rates_run = rates_seed
    rates_parts = lax.all_to_all(
        jnp.broadcast_to(rates_run, (pieces,) + left_rates.shape), "sub", 0, 0, tiled=True
    )
    rates_full = jnp.moveaxis(rates_parts, 0, 1).reshape(local_blocks, width_two)
    partial = jnp.einsum(
        "tab,ktbc->kac", left_part, right_done, preferred_element_type=jnp.float32
    ).astype(jnp.bfloat16)
    dual_cols = jnp.einsum(
        "jab,jbc->jac", left_dual, partial, preferred_element_type=jnp.float32
    ).astype(jnp.bfloat16)
    mixed = jnp.einsum("jrn,jmn->jrm", dual_cols, right_dual, preferred_element_type=jnp.float32)
    scaled = (mixed / (rates_full[:, :, None] + right_rates[:, None, :])).astype(jnp.bfloat16)
    basis_rows = jnp.einsum(
        "jrm,jkm->jrk", scaled, right_eigenvector_matrix, preferred_element_type=jnp.float32
    ).astype(jnp.bfloat16)
    basis_rows = basis_rows.reshape(local_blocks, width_two, pieces, cols)
    spread = jnp.einsum(
        "jab,jbkc->kjac", left_basis, basis_rows, preferred_element_type=jnp.float32
    ).astype(jnp.bfloat16)
    return scatter_sum(spread, "sub")


def solution(mesh):
    placed = (
        P("blk", "sub", None),
        P(),
        P(),
        P(),
        P(),
        P("blk", None, None),
        P("blk", None, None),
        P("blk", None, None),
        P("blk", None, None),
        P("blk", "sub"),
        P("blk", None),
    )
    return jax.shard_map(
        local, mesh=mesh, in_specs=placed, out_specs=P("blk", None, "sub"), check_vma=False
    )
```

```python
import jax
import jax.numpy as jnp
from jax import lax
from jax.sharding import PartitionSpec as P


def scatter_sum(chunks, axis):
    n = chunks.shape[0]
    me = lax.axis_index(axis)
    total = lax.dynamic_index_in_dim(chunks, me, 0, keepdims=False).astype(jnp.float32)
    for k in range(1, n):
        send = lax.dynamic_index_in_dim(chunks, (me + k) % n, 0, keepdims=False)
        got = lax.ppermute(send, axis, [(j, (j + k) % n) for j in range(n)])
        total = total + got.astype(jnp.float32)
    return total


def local(
    block_vec,
    left_factor,
    right_factor,
    pairs,
    pair_count,
    left_basis,
    left_dual,
    right_eigenvector_matrix,
    right_dual,
    left_rates,
    right_rates,
):
    owner = lax.axis_index("blk")
    part = lax.axis_index("sub")
    groups = lax.axis_size("blk")
    pieces = lax.axis_size("sub")
    local_blocks = block_vec.shape[0]
    row_count = block_vec.shape[1]
    width_two = block_vec.shape[2]
    slots_per = pairs.shape[2]
    term_total = left_factor.shape[0]
    all_count = groups * local_blocks
    cols = width_two // pieces
    incoming = lax.dynamic_index_in_dim(pairs, owner, 1, keepdims=False)
    counts = lax.dynamic_index_in_dim(pair_count, owner, 1, keepdims=False)
    live_mask = (jnp.arange(slots_per)[None, :] < counts[:, None]).astype(jnp.float32)
    target_term = incoming[..., 1] * term_total + incoming[..., 2]
    source = jnp.arange(groups, dtype=jnp.int32)[:, None] * local_blocks + incoming[..., 0]
    key_onehot = (
        target_term[..., None] == jnp.arange(local_blocks * term_total)[None, None, :]
    ).astype(jnp.float32) * live_mask[..., None]
    ring = 4
    core = owner % 2
    here_x = owner // (2 * ring)
    here_y = (owner // 2) % ring
    offsets = jnp.arange(ring, dtype=jnp.int32)
    plane_group = (((here_x + offsets[None, :]) % ring) * ring + (here_y + offsets[:, None]) % ring) * 2
    side_group = plane_group[None] + jnp.stack([core, 1 - core])[:, None, None]
    block_ids = (side_group[..., None] * local_blocks + jnp.arange(local_blocks)).reshape(-1)
    source_onehot = (source[..., None] == block_ids[None, None, :]).astype(jnp.float32)
    weights = jnp.einsum("gqk,gqs->ks", key_onehot, source_onehot).astype(jnp.bfloat16)
    weights = weights.reshape(local_blocks * term_total, 2, ring, ring, local_blocks)

    def move(piece, dx, dy, sibling=False):
        pairs_list = []
        for b in range(groups):
            bx, by, bc = b // (2 * ring), (b // 2) % ring, b % 2
            if sibling:
                dest = b ^ 1
            else:
                dest = (((bx + dx) % ring) * ring + (by + dy) % ring) * 2 + bc
            pairs_list.append((b, dest))
        return lax.ppermute(piece, "blk", pairs_list)

    half_blocks = local_blocks // 2
    from_left = move(block_vec, 1, 0)
    from_right = move(block_vec, -1, 0)
    far = jnp.concatenate(
        [move(from_left[:half_blocks], 1, 0), move(from_right[half_blocks:], -1, 0)], axis=0
    )
    x_row = jnp.stack([block_vec, from_right, far, from_left])
    side_x = move(x_row, 0, 0, sibling=True)
    from_below = move(x_row, 0, 1)
    from_above = move(x_row, 0, -1)
    side_above = move(from_above, 0, 0, sibling=True)
    side_below = move(from_below, 0, 0, sibling=True)
    half_ring = ring // 2
    far_y = jnp.concatenate(
        [move(from_below[:half_ring], 0, 1), move(from_above[half_ring:], 0, -1)], axis=0
    )
    side_far = move(far_y, 0, 0, sibling=True)

    def pool(w, piece):
        return jnp.einsum("kab,abrn->krn", w, piece, preferred_element_type=jnp.float32)

    pooled = (
        pool(weights[:, 0, 0], x_row)
        + pool(weights[:, 0, 1], from_above)
        + pool(weights[:, 0, 2], far_y)
        + pool(weights[:, 0, 3], from_below)
        + pool(weights[:, 1, 0], side_x)
        + pool(weights[:, 1, 1], side_above)
        + pool(weights[:, 1, 2], side_far)
        + pool(weights[:, 1, 3], side_below)
    ).astype(jnp.bfloat16)
    pooled = pooled.reshape(local_blocks, term_total, row_count, width_two)
    right_done = jnp.einsum(
        "ktrn,tmn->ktrm", pooled, right_factor, preferred_element_type=jnp.float32
    ).astype(jnp.bfloat16)
    left_part = lax.dynamic_slice_in_dim(left_factor, part * row_count, row_count, axis=2)
    rates_run = left_rates[None]
    rates_parts = lax.all_to_all(
        jnp.broadcast_to(rates_run, (pieces,) + left_rates.shape), "sub", 0, 0, tiled=True
    )
    rates_full = jnp.moveaxis(rates_parts, 0, 1).reshape(local_blocks, width_two)
    left_flat = jnp.transpose(left_part, (1, 0, 2)).reshape(width_two, term_total * row_count)
    done_flat = right_done.reshape(local_blocks, term_total * row_count, width_two)
    left_flat, done_flat = lax.optimization_barrier((left_flat, done_flat))
    partial = jnp.einsum(
        "ak,jkc->jac", left_flat, done_flat, preferred_element_type=jnp.float32
    ).astype(jnp.bfloat16)
    dual_cols = jnp.einsum(
        "jab,jbc->jac", left_dual, partial, preferred_element_type=jnp.float32
    ).astype(jnp.bfloat16)
    mixed = jnp.einsum("jrn,jmn->jrm", dual_cols, right_dual, preferred_element_type=jnp.float32)
    scaled = (mixed / (rates_full[:, :, None] + right_rates[:, None, :])).astype(jnp.bfloat16)
    basis_rows = jnp.einsum(
        "jrm,jkm->jrk", scaled, right_eigenvector_matrix, preferred_element_type=jnp.float32
    ).astype(jnp.bfloat16)
    basis_rows = basis_rows.reshape(local_blocks, width_two, pieces, cols)
    spread = jnp.einsum(
        "jab,jbkc->kjac", left_basis, basis_rows, preferred_element_type=jnp.float32
    ).astype(jnp.bfloat16)
    return scatter_sum(spread, "sub")


def solution(mesh):
    placed = (
        P("blk", "sub", None),
        P(),
        P(),
        P(),
        P(),
        P("blk", None, None),
        P("blk", None, None),
        P("blk", None, None),
        P("blk", None, None),
        P("blk", "sub"),
        P("blk", None),
    )
    return jax.shard_map(
        local, mesh=mesh, in_specs=placed, out_specs=P("blk", None, "sub"), check_vma=False
    )
```

```python
import jax
import jax.numpy as jnp
from jax import lax
from jax.sharding import PartitionSpec as P


def scatter_sum(chunks, axis):
    n = chunks.shape[0]
    me = lax.axis_index(axis)
    total = lax.dynamic_index_in_dim(chunks, me, 0, keepdims=False).astype(jnp.float32)
    for k in sorted(range(1, n), key=lambda k: (-min(k, n - k), k)):
        send = lax.dynamic_index_in_dim(chunks, (me + k) % n, 0, keepdims=False)
        got = lax.ppermute(send, axis, [(j, (j + k) % n) for j in range(n)])
        total = total + got.astype(jnp.float32)
    return total


def local(
    block_vec,
    left_factor,
    right_factor,
    pairs,
    pair_count,
    left_basis,
    left_dual,
    right_eigenvector_matrix,
    right_dual,
    left_rates,
    right_rates,
):
    owner = lax.axis_index("blk")
    part = lax.axis_index("sub")
    groups = lax.axis_size("blk")
    pieces = lax.axis_size("sub")
    local_blocks = block_vec.shape[0]
    row_count = block_vec.shape[1]
    width_two = block_vec.shape[2]
    slots_per = pairs.shape[2]
    term_total = left_factor.shape[0]
    all_count = groups * local_blocks
    cols = width_two // pieces
    incoming = lax.dynamic_index_in_dim(pairs, owner, 1, keepdims=False)
    counts = lax.dynamic_index_in_dim(pair_count, owner, 1, keepdims=False)
    live_mask = (jnp.arange(slots_per)[None, :] < counts[:, None]).astype(jnp.float32)
    target_term = incoming[..., 1] * term_total + incoming[..., 2]
    source = jnp.arange(groups, dtype=jnp.int32)[:, None] * local_blocks + incoming[..., 0]
    key_onehot = (
        target_term[..., None] == jnp.arange(local_blocks * term_total)[None, None, :]
    ).astype(jnp.float32) * live_mask[..., None]
    ring = 4
    core = owner % 2
    here_x = owner // (2 * ring)
    here_y = (owner // 2) % ring
    offsets = jnp.arange(ring, dtype=jnp.int32)
    plane_group = (((here_x + offsets[None, :]) % ring) * ring + (here_y + offsets[:, None]) % ring) * 2
    side_group = plane_group[None] + jnp.stack([core, 1 - core])[:, None, None]
    block_ids = (side_group[..., None] * local_blocks + jnp.arange(local_blocks)).reshape(-1)
    source_onehot = (source[..., None] == block_ids[None, None, :]).astype(jnp.float32)
    weights = jnp.einsum("gqk,gqs->ks", key_onehot, source_onehot).astype(jnp.bfloat16)
    weights = weights.reshape(local_blocks * term_total, 2, ring, ring, local_blocks)

    def move(piece, dx, dy, sibling=False):
        pairs_list = []
        for b in range(groups):
            bx, by, bc = b // (2 * ring), (b // 2) % ring, b % 2
            if sibling:
                dest = b ^ 1
            else:
                dest = (((bx + dx) % ring) * ring + (by + dy) % ring) * 2 + bc
            pairs_list.append((b, dest))
        return lax.ppermute(piece, "blk", pairs_list)

    half_blocks = local_blocks // 2
    from_left = move(block_vec, 1, 0)
    from_right = move(block_vec, -1, 0)
    far = jnp.concatenate(
        [move(from_left[:half_blocks], 1, 0), move(from_right[half_blocks:], -1, 0)], axis=0
    )
    x_row = jnp.stack([block_vec, from_right, far, from_left])
    side_x = move(x_row, 0, 0, sibling=True)
    from_below = move(x_row, 0, 1)
    from_above = move(x_row, 0, -1)
    side_above = move(from_above, 0, 0, sibling=True)
    side_below = move(from_below, 0, 0, sibling=True)
    half_ring = ring // 2
    far_y = jnp.concatenate(
        [move(from_below[:half_ring], 0, 1), move(from_above[half_ring:], 0, -1)], axis=0
    )
    side_far = move(far_y, 0, 0, sibling=True)

    def pool(w, piece):
        return jnp.einsum("kab,abrn->krn", w, piece, preferred_element_type=jnp.float32)

    pooled = (
        pool(weights[:, 0, 0], x_row)
        + pool(weights[:, 0, 1], from_above)
        + pool(weights[:, 0, 2], far_y)
        + pool(weights[:, 0, 3], from_below)
        + pool(weights[:, 1, 0], side_x)
        + pool(weights[:, 1, 1], side_above)
        + pool(weights[:, 1, 2], side_far)
        + pool(weights[:, 1, 3], side_below)
    ).astype(jnp.bfloat16)
    pooled = pooled.reshape(local_blocks, term_total, row_count, width_two)
    right_done = jnp.einsum(
        "ktrn,tmn->ktrm", pooled, right_factor, preferred_element_type=jnp.float32
    ).astype(jnp.bfloat16)
    left_part = lax.dynamic_slice_in_dim(left_factor, part * row_count, row_count, axis=2)
    rates_run = left_rates[None]
    rates_parts = lax.all_to_all(
        jnp.broadcast_to(rates_run, (pieces,) + left_rates.shape), "sub", 0, 0, tiled=True
    )
    rates_full = jnp.moveaxis(rates_parts, 0, 1).reshape(local_blocks, width_two)
    partial = jnp.einsum(
        "tab,ktbc->kac", left_part, right_done, preferred_element_type=jnp.float32
    ).astype(jnp.bfloat16)
    dual_cols = jnp.einsum(
        "jab,jbc->jac", left_dual, partial, preferred_element_type=jnp.float32
    ).astype(jnp.bfloat16)
    mixed = jnp.einsum("jrn,jmn->jrm", dual_cols, right_dual, preferred_element_type=jnp.float32)
    scaled = (mixed / (rates_full[:, :, None] + right_rates[:, None, :])).astype(jnp.bfloat16)
    basis_rows = jnp.einsum(
        "jrm,jkm->jrk", scaled, right_eigenvector_matrix, preferred_element_type=jnp.float32
    ).astype(jnp.bfloat16)
    basis_rows = basis_rows.reshape(local_blocks, width_two, pieces, cols)
    spread = jnp.einsum(
        "jab,jbkc->kjac", left_basis, basis_rows, preferred_element_type=jnp.float32
    ).astype(jnp.bfloat16)
    return scatter_sum(spread, "sub")


def solution(mesh):
    placed = (
        P("blk", "sub", None),
        P(),
        P(),
        P(),
        P(),
        P("blk", None, None),
        P("blk", None, None),
        P("blk", None, None),
        P("blk", None, None),
        P("blk", "sub"),
        P("blk", None),
    )
    return jax.shard_map(
        local, mesh=mesh, in_specs=placed, out_specs=P("blk", None, "sub"), check_vma=False
    )
```

```python
import jax
import jax.numpy as jnp
from jax import lax
from jax.sharding import PartitionSpec as P


def scatter_sum(make_chunk, n, axis):
    me = lax.axis_index(axis)
    total = None
    for k in sorted(range(1, n), key=lambda k: (-min(k, n - k), k)):
        send = make_chunk((me + k) % n)
        got = lax.ppermute(send, axis, [(j, (j + k) % n) for j in range(n)])
        total = got.astype(jnp.float32) if total is None else total + got.astype(jnp.float32)
    return total + make_chunk(me).astype(jnp.float32)


def local(
    block_vec,
    left_factor,
    right_factor,
    pairs,
    pair_count,
    left_basis,
    left_dual,
    right_eigenvector_matrix,
    right_dual,
    left_rates,
    right_rates,
):
    owner = lax.axis_index("blk")
    part = lax.axis_index("sub")
    groups = lax.axis_size("blk")
    pieces = lax.axis_size("sub")
    local_blocks = block_vec.shape[0]
    row_count = block_vec.shape[1]
    width_two = block_vec.shape[2]
    slots_per = pairs.shape[2]
    term_total = left_factor.shape[0]
    all_count = groups * local_blocks
    cols = width_two // pieces
    incoming = lax.dynamic_index_in_dim(pairs, owner, 1, keepdims=False)
    counts = lax.dynamic_index_in_dim(pair_count, owner, 1, keepdims=False)
    live_mask = (jnp.arange(slots_per)[None, :] < counts[:, None]).astype(jnp.float32)
    target_term = incoming[..., 1] * term_total + incoming[..., 2]
    source = jnp.arange(groups, dtype=jnp.int32)[:, None] * local_blocks + incoming[..., 0]
    key_onehot = (
        target_term[..., None] == jnp.arange(local_blocks * term_total)[None, None, :]
    ).astype(jnp.float32) * live_mask[..., None]
    ring = 4
    core = owner % 2
    here_x = owner // (2 * ring)
    here_y = (owner // 2) % ring
    offsets = jnp.arange(ring, dtype=jnp.int32)
    plane_group = (((here_x + offsets[None, :]) % ring) * ring + (here_y + offsets[:, None]) % ring) * 2
    side_group = plane_group[None] + jnp.stack([core, 1 - core])[:, None, None]
    block_ids = (side_group[..., None] * local_blocks + jnp.arange(local_blocks)).reshape(-1)
    source_onehot = (source[..., None] == block_ids[None, None, :]).astype(jnp.float32)
    weights = jnp.einsum("gqk,gqs->ks", key_onehot, source_onehot).astype(jnp.bfloat16)
    weights = weights.reshape(local_blocks * term_total, 2, ring, ring, local_blocks)

    def move(piece, dx, dy, sibling=False):
        pairs_list = []
        for b in range(groups):
            bx, by, bc = b // (2 * ring), (b // 2) % ring, b % 2
            if sibling:
                dest = b ^ 1
            else:
                dest = (((bx + dx) % ring) * ring + (by + dy) % ring) * 2 + bc
            pairs_list.append((b, dest))
        return lax.ppermute(piece, "blk", pairs_list)

    half_blocks = local_blocks // 2
    from_left = move(block_vec, 1, 0)
    from_right = move(block_vec, -1, 0)
    far = jnp.concatenate(
        [move(from_left[:half_blocks], 1, 0), move(from_right[half_blocks:], -1, 0)], axis=0
    )
    x_row = jnp.stack([block_vec, from_right, far, from_left])
    side_x = move(x_row, 0, 0, sibling=True)
    from_below = move(x_row, 0, 1)
    from_above = move(x_row, 0, -1)
    side_above = move(from_above, 0, 0, sibling=True)
    side_below = move(from_below, 0, 0, sibling=True)
    half_ring = ring // 2
    far_y = jnp.concatenate(
        [move(from_below[:half_ring], 0, 1), move(from_above[half_ring:], 0, -1)], axis=0
    )
    side_far = move(far_y, 0, 0, sibling=True)

    def pool(w, piece):
        return jnp.einsum("kab,abrn->krn", w, piece, preferred_element_type=jnp.float32)

    pooled = (
        pool(weights[:, 0, 0], x_row)
        + pool(weights[:, 0, 1], from_above)
        + pool(weights[:, 0, 2], far_y)
        + pool(weights[:, 0, 3], from_below)
        + pool(weights[:, 1, 0], side_x)
        + pool(weights[:, 1, 1], side_above)
        + pool(weights[:, 1, 2], side_far)
        + pool(weights[:, 1, 3], side_below)
    ).astype(jnp.bfloat16)
    pooled = pooled.reshape(local_blocks, term_total, row_count, width_two)
    right_done = jnp.einsum(
        "ktrn,tmn->ktrm", pooled, right_factor, preferred_element_type=jnp.float32
    ).astype(jnp.bfloat16)
    left_part = lax.dynamic_slice_in_dim(left_factor, part * row_count, row_count, axis=2)
    rates_run = left_rates[None]
    rates_parts = lax.all_to_all(
        jnp.broadcast_to(rates_run, (pieces,) + left_rates.shape), "sub", 0, 0, tiled=True
    )
    rates_full = jnp.moveaxis(rates_parts, 0, 1).reshape(local_blocks, width_two)
    partial = jnp.einsum(
        "tab,ktbc->kac", left_part, right_done, preferred_element_type=jnp.float32
    ).astype(jnp.bfloat16)
    dual_cols = jnp.einsum(
        "jab,jbc->jac", left_dual, partial, preferred_element_type=jnp.float32
    ).astype(jnp.bfloat16)
    mixed = jnp.einsum("jrn,jmn->jrm", dual_cols, right_dual, preferred_element_type=jnp.float32)
    scaled = (mixed / (rates_full[:, :, None] + right_rates[:, None, :])).astype(jnp.bfloat16)
    basis_rows = jnp.einsum(
        "jrm,jkm->jrk", scaled, right_eigenvector_matrix, preferred_element_type=jnp.float32
    ).astype(jnp.bfloat16)

    def make_chunk(idx):
        piece = lax.dynamic_slice_in_dim(basis_rows, idx * cols, cols, axis=2)
        return jnp.einsum(
            "jab,jbc->jac", left_basis, piece, preferred_element_type=jnp.float32
        ).astype(jnp.bfloat16)

    return scatter_sum(make_chunk, pieces, "sub")


def solution(mesh):
    placed = (
        P("blk", "sub", None),
        P(),
        P(),
        P(),
        P(),
        P("blk", None, None),
        P("blk", None, None),
        P("blk", None, None),
        P("blk", None, None),
        P("blk", "sub"),
        P("blk", None),
    )
    return jax.shard_map(
        local, mesh=mesh, in_specs=placed, out_specs=P("blk", None, "sub"), check_vma=False
    )
```

```python
import jax
import jax.numpy as jnp
from jax import lax
from jax.sharding import PartitionSpec as P


def scatter_sum(make_chunk, n, axis):
    me = lax.axis_index(axis)
    total = None
    for k in sorted(range(1, n), key=lambda k: (-min(k, n - k), k)):
        send = make_chunk((me + k) % n)
        got = lax.ppermute(send, axis, [(j, (j + k) % n) for j in range(n)])
        total = got.astype(jnp.float32) if total is None else total + got.astype(jnp.float32)
    return total + make_chunk(me).astype(jnp.float32)


def local(
    block_vec,
    left_factor,
    right_factor,
    pairs,
    pair_count,
    left_basis,
    left_dual,
    right_eigenvector_matrix,
    right_dual,
    left_rates,
    right_rates,
):
    owner = lax.axis_index("blk")
    part = lax.axis_index("sub")
    groups = lax.axis_size("blk")
    pieces = lax.axis_size("sub")
    local_blocks = block_vec.shape[0]
    row_count = block_vec.shape[1]
    width_two = block_vec.shape[2]
    slots_per = pairs.shape[2]
    term_total = left_factor.shape[0]
    all_count = groups * local_blocks
    cols = width_two // pieces
    incoming = lax.dynamic_index_in_dim(pairs, owner, 1, keepdims=False)
    counts = lax.dynamic_index_in_dim(pair_count, owner, 1, keepdims=False)
    live_mask = (jnp.arange(slots_per)[None, :] < counts[:, None]).astype(jnp.float32)
    target_term = incoming[..., 1] * term_total + incoming[..., 2]
    source = jnp.arange(groups, dtype=jnp.int32)[:, None] * local_blocks + incoming[..., 0]
    key_onehot = (
        target_term[..., None] == jnp.arange(local_blocks * term_total)[None, None, :]
    ).astype(jnp.float32) * live_mask[..., None]
    ring = 4
    core = owner % 2
    here_x = owner // (2 * ring)
    here_y = (owner // 2) % ring
    offsets = jnp.arange(ring, dtype=jnp.int32)
    plane_group = (((here_x + offsets[None, :]) % ring) * ring + (here_y + offsets[:, None]) % ring) * 2
    side_group = plane_group[None] + jnp.stack([core, 1 - core])[:, None, None]
    block_ids = (side_group[..., None] * local_blocks + jnp.arange(local_blocks)).reshape(-1)
    source_onehot = (source[..., None] == block_ids[None, None, :]).astype(jnp.float32)
    weights = jnp.einsum("gqk,gqs->ks", key_onehot, source_onehot).astype(jnp.bfloat16)
    weights = weights.reshape(local_blocks * term_total, 2, ring, ring, local_blocks)

    def move(piece, dx, dy, sibling=False):
        pairs_list = []
        for b in range(groups):
            bx, by, bc = b // (2 * ring), (b // 2) % ring, b % 2
            if sibling:
                dest = b ^ 1
            else:
                dest = (((bx + dx) % ring) * ring + (by + dy) % ring) * 2 + bc
            pairs_list.append((b, dest))
        return lax.ppermute(piece, "blk", pairs_list)

    half_blocks = local_blocks // 2
    from_left = move(block_vec, 1, 0)
    from_right = move(block_vec, -1, 0)
    far = jnp.concatenate(
        [move(from_left[:half_blocks], 1, 0), move(from_right[half_blocks:], -1, 0)], axis=0
    )
    x_row = jnp.stack([block_vec, from_right, far, from_left])
    side_x = move(x_row, 0, 0, sibling=True)
    from_below = move(x_row, 0, 1)
    from_above = move(x_row, 0, -1)
    side_above = move(from_above, 0, 0, sibling=True)
    side_below = move(from_below, 0, 0, sibling=True)
    half_ring = ring // 2
    far_low = move(from_below[:half_ring], 0, 1)
    far_high = move(from_above[half_ring:], 0, -1)
    side_low = move(far_low, 0, 0, sibling=True)
    side_high = move(far_high, 0, 0, sibling=True)

    def pool(w, piece):
        return jnp.einsum("kab,abrn->krn", w, piece, preferred_element_type=jnp.float32)

    pooled = (
        pool(weights[:, 0, 0], x_row)
        + pool(weights[:, 0, 1], from_above)
        + pool(weights[:, 0, 2, :half_ring], far_low)
        + pool(weights[:, 0, 2, half_ring:], far_high)
        + pool(weights[:, 0, 3], from_below)
        + pool(weights[:, 1, 0], side_x)
        + pool(weights[:, 1, 1], side_above)
        + pool(weights[:, 1, 2, :half_ring], side_low)
        + pool(weights[:, 1, 2, half_ring:], side_high)
        + pool(weights[:, 1, 3], side_below)
    ).astype(jnp.bfloat16)
    pooled = pooled.reshape(local_blocks, term_total, row_count, width_two)
    right_done = jnp.einsum(
        "ktrn,tmn->ktrm", pooled, right_factor, preferred_element_type=jnp.float32
    ).astype(jnp.bfloat16)
    left_part = lax.dynamic_slice_in_dim(left_factor, part * row_count, row_count, axis=2)
    rates_run = left_rates[None]
    rates_parts = lax.all_to_all(
        jnp.broadcast_to(rates_run, (pieces,) + left_rates.shape), "sub", 0, 0, tiled=True
    )
    rates_full = jnp.moveaxis(rates_parts, 0, 1).reshape(local_blocks, width_two)
    partial = jnp.einsum(
        "tab,ktbc->kac", left_part, right_done, preferred_element_type=jnp.float32
    ).astype(jnp.bfloat16)
    dual_cols = jnp.einsum(
        "jab,jbc->jac", left_dual, partial, preferred_element_type=jnp.float32
    ).astype(jnp.bfloat16)
    mixed = jnp.einsum("jrn,jmn->jrm", dual_cols, right_dual, preferred_element_type=jnp.float32)
    scaled = (mixed / (rates_full[:, :, None] + right_rates[:, None, :])).astype(jnp.bfloat16)
    basis_rows = jnp.einsum(
        "jrm,jkm->jrk", scaled, right_eigenvector_matrix, preferred_element_type=jnp.float32
    ).astype(jnp.bfloat16)

    def make_chunk(idx):
        piece = lax.dynamic_slice_in_dim(basis_rows, idx * cols, cols, axis=2)
        return jnp.einsum(
            "jab,jbc->jac", left_basis, piece, preferred_element_type=jnp.float32
        ).astype(jnp.bfloat16)

    return scatter_sum(make_chunk, pieces, "sub")


def solution(mesh):
    placed = (
        P("blk", "sub", None),
        P(),
        P(),
        P(),
        P(),
        P("blk", None, None),
        P("blk", None, None),
        P("blk", None, None),
        P("blk", None, None),
        P("blk", "sub"),
        P("blk", None),
    )
    return jax.shard_map(
        local, mesh=mesh, in_specs=placed, out_specs=P("blk", None, "sub"), check_vma=False
    )
```

```python
import jax
import jax.numpy as jnp
from jax import lax
from jax.sharding import PartitionSpec as P


def scatter_sum(make_chunk, n, axis):
    me = lax.axis_index(axis)
    total = None
    for k in [n // 2] + list(range(n // 2 - 1, 0, -1)) + list(range(n // 2 + 1, n)):
        send = make_chunk((me + k) % n)
        got = lax.ppermute(send, axis, [(j, (j + k) % n) for j in range(n)])
        total = got.astype(jnp.float32) if total is None else total + got.astype(jnp.float32)
    return total + make_chunk(me).astype(jnp.float32)


def local(
    block_vec,
    left_factor,
    right_factor,
    pairs,
    pair_count,
    left_basis,
    left_dual,
    right_eigenvector_matrix,
    right_dual,
    left_rates,
    right_rates,
):
    owner = lax.axis_index("blk")
    part = lax.axis_index("sub")
    groups = lax.axis_size("blk")
    pieces = lax.axis_size("sub")
    local_blocks = block_vec.shape[0]
    row_count = block_vec.shape[1]
    width_two = block_vec.shape[2]
    slots_per = pairs.shape[2]
    term_total = left_factor.shape[0]
    all_count = groups * local_blocks
    cols = width_two // pieces
    incoming = lax.dynamic_index_in_dim(pairs, owner, 1, keepdims=False)
    counts = lax.dynamic_index_in_dim(pair_count, owner, 1, keepdims=False)
    live_mask = (jnp.arange(slots_per)[None, :] < counts[:, None]).astype(jnp.float32)
    target_term = incoming[..., 1] * term_total + incoming[..., 2]
    source = jnp.arange(groups, dtype=jnp.int32)[:, None] * local_blocks + incoming[..., 0]
    key_onehot = (
        target_term[..., None] == jnp.arange(local_blocks * term_total)[None, None, :]
    ).astype(jnp.float32) * live_mask[..., None]
    ring = 4
    core = owner % 2
    here_x = owner // (2 * ring)
    here_y = (owner // 2) % ring
    offsets = jnp.arange(ring, dtype=jnp.int32)
    plane_group = (((here_x + offsets[None, :]) % ring) * ring + (here_y + offsets[:, None]) % ring) * 2
    side_group = plane_group[None] + jnp.stack([core, 1 - core])[:, None, None]
    block_ids = (side_group[..., None] * local_blocks + jnp.arange(local_blocks)).reshape(-1)
    source_onehot = (source[..., None] == block_ids[None, None, :]).astype(jnp.float32)
    weights = jnp.einsum("gqk,gqs->ks", key_onehot, source_onehot).astype(jnp.bfloat16)
    weights = weights.reshape(local_blocks * term_total, 2, ring, ring, local_blocks)

    def move(piece, dx, dy, sibling=False):
        pairs_list = []
        for b in range(groups):
            bx, by, bc = b // (2 * ring), (b // 2) % ring, b % 2
            if sibling:
                dest = b ^ 1
            else:
                dest = (((bx + dx) % ring) * ring + (by + dy) % ring) * 2 + bc
            pairs_list.append((b, dest))
        return lax.ppermute(piece, "blk", pairs_list)

    half_blocks = local_blocks // 2
    from_left = move(block_vec, 1, 0)
    from_right = move(block_vec, -1, 0)
    far = jnp.concatenate(
        [move(from_left[:half_blocks], 1, 0), move(from_right[half_blocks:], -1, 0)], axis=0
    )
    x_row = jnp.stack([block_vec, from_right, far, from_left])
    side_x = move(x_row, 0, 0, sibling=True)
    from_below = move(x_row, 0, 1)
    from_above = move(x_row, 0, -1)
    side_above = move(from_above, 0, 0, sibling=True)
    side_below = move(from_below, 0, 0, sibling=True)
    half_ring = ring // 2
    far_y = jnp.concatenate(
        [move(from_below[:half_ring], 0, 1), move(from_above[half_ring:], 0, -1)], axis=0
    )
    side_far = move(far_y, 0, 0, sibling=True)

    def pool(w, piece):
        return jnp.einsum("kab,abrn->krn", w, piece, preferred_element_type=jnp.float32)

    pooled = (
        pool(weights[:, 0, 0], x_row)
        + pool(weights[:, 0, 1], from_above)
        + pool(weights[:, 0, 2], far_y)
        + pool(weights[:, 0, 3], from_below)
        + pool(weights[:, 1, 0], side_x)
        + pool(weights[:, 1, 1], side_above)
        + pool(weights[:, 1, 2], side_far)
        + pool(weights[:, 1, 3], side_below)
    ).astype(jnp.bfloat16)
    pooled = pooled.reshape(local_blocks, term_total, row_count, width_two)
    right_done = jnp.einsum(
        "ktrn,tmn->ktrm", pooled, right_factor, preferred_element_type=jnp.float32
    ).astype(jnp.bfloat16)
    left_part = lax.dynamic_slice_in_dim(left_factor, part * row_count, row_count, axis=2)
    rates_run = left_rates[None]
    rates_parts = lax.all_to_all(
        jnp.broadcast_to(rates_run, (pieces,) + left_rates.shape), "sub", 0, 0, tiled=True
    )
    rates_full = jnp.moveaxis(rates_parts, 0, 1).reshape(local_blocks, width_two)
    partial = jnp.einsum(
        "tab,ktbc->kac", left_part, right_done, preferred_element_type=jnp.float32
    ).astype(jnp.bfloat16)
    dual_cols = jnp.einsum(
        "jab,jbc->jac", left_dual, partial, preferred_element_type=jnp.float32
    ).astype(jnp.bfloat16)
    mixed = jnp.einsum("jrn,jmn->jrm", dual_cols, right_dual, preferred_element_type=jnp.float32)
    scaled = (mixed / (rates_full[:, :, None] + right_rates[:, None, :])).astype(jnp.bfloat16)
    basis_rows = jnp.einsum(
        "jrm,jkm->jrk", scaled, right_eigenvector_matrix, preferred_element_type=jnp.float32
    ).astype(jnp.bfloat16)

    def make_chunk(idx):
        piece = lax.dynamic_slice_in_dim(basis_rows, idx * cols, cols, axis=2)
        return jnp.einsum(
            "jab,jbc->jac", left_basis, piece, preferred_element_type=jnp.float32
        ).astype(jnp.bfloat16)

    return scatter_sum(make_chunk, pieces, "sub")


def solution(mesh):
    placed = (
        P("blk", "sub", None),
        P(),
        P(),
        P(),
        P(),
        P("blk", None, None),
        P("blk", None, None),
        P("blk", None, None),
        P("blk", None, None),
        P("blk", "sub"),
        P("blk", None),
    )
    return jax.shard_map(
        local, mesh=mesh, in_specs=placed, out_specs=P("blk", None, "sub"), check_vma=False
    )
```

```python
import jax
import jax.numpy as jnp
from jax import lax
from jax.sharding import PartitionSpec as P


def scatter_sum(make_chunk, n, axis):
    me = lax.axis_index(axis)
    total = None
    for k in sorted(range(1, n), key=lambda k: (-min(k, n - k), k)):
        send = make_chunk((me + k) % n)
        got = lax.ppermute(send, axis, [(j, (j + k) % n) for j in range(n)])
        total = got.astype(jnp.float32) if total is None else total + got.astype(jnp.float32)
        total = lax.optimization_barrier(total)
    return total + make_chunk(me).astype(jnp.float32)


def local(
    block_vec,
    left_factor,
    right_factor,
    pairs,
    pair_count,
    left_basis,
    left_dual,
    right_eigenvector_matrix,
    right_dual,
    left_rates,
    right_rates,
):
    owner = lax.axis_index("blk")
    part = lax.axis_index("sub")
    groups = lax.axis_size("blk")
    pieces = lax.axis_size("sub")
    local_blocks = block_vec.shape[0]
    row_count = block_vec.shape[1]
    width_two = block_vec.shape[2]
    slots_per = pairs.shape[2]
    term_total = left_factor.shape[0]
    all_count = groups * local_blocks
    cols = width_two // pieces
    incoming = lax.dynamic_index_in_dim(pairs, owner, 1, keepdims=False)
    counts = lax.dynamic_index_in_dim(pair_count, owner, 1, keepdims=False)
    live_mask = (jnp.arange(slots_per)[None, :] < counts[:, None]).astype(jnp.float32)
    target_term = incoming[..., 1] * term_total + incoming[..., 2]
    source = jnp.arange(groups, dtype=jnp.int32)[:, None] * local_blocks + incoming[..., 0]
    key_onehot = (
        target_term[..., None] == jnp.arange(local_blocks * term_total)[None, None, :]
    ).astype(jnp.float32) * live_mask[..., None]
    ring = 4
    core = owner % 2
    here_x = owner // (2 * ring)
    here_y = (owner // 2) % ring
    offsets = jnp.arange(ring, dtype=jnp.int32)
    plane_group = (((here_x + offsets[None, :]) % ring) * ring + (here_y + offsets[:, None]) % ring) * 2
    side_group = plane_group[None] + jnp.stack([core, 1 - core])[:, None, None]
    block_ids = (side_group[..., None] * local_blocks + jnp.arange(local_blocks)).reshape(-1)
    source_onehot = (source[..., None] == block_ids[None, None, :]).astype(jnp.float32)
    weights = jnp.einsum("gqk,gqs->ks", key_onehot, source_onehot).astype(jnp.bfloat16)
    weights = weights.reshape(local_blocks * term_total, 2, ring, ring, local_blocks)

    def move(piece, dx, dy, sibling=False):
        pairs_list = []
        for b in range(groups):
            bx, by, bc = b // (2 * ring), (b // 2) % ring, b % 2
            if sibling:
                dest = b ^ 1
            else:
                dest = (((bx + dx) % ring) * ring + (by + dy) % ring) * 2 + bc
            pairs_list.append((b, dest))
        return lax.ppermute(piece, "blk", pairs_list)

    half_blocks = local_blocks // 2
    from_left = move(block_vec, 1, 0)
    from_right = move(block_vec, -1, 0)
    far = jnp.concatenate(
        [move(from_left[:half_blocks], 1, 0), move(from_right[half_blocks:], -1, 0)], axis=0
    )
    x_row = jnp.stack([block_vec, from_right, far, from_left])
    side_x = move(x_row, 0, 0, sibling=True)
    from_below = move(x_row, 0, 1)
    from_above = move(x_row, 0, -1)
    side_above = move(from_above, 0, 0, sibling=True)
    side_below = move(from_below, 0, 0, sibling=True)
    half_ring = ring // 2
    far_y = jnp.concatenate(
        [move(from_below[:half_ring], 0, 1), move(from_above[half_ring:], 0, -1)], axis=0
    )
    side_far = move(far_y, 0, 0, sibling=True)

    def pool(w, piece):
        return jnp.einsum("kab,abrn->krn", w, piece, preferred_element_type=jnp.float32)

    pooled = (
        pool(weights[:, 0, 0], x_row)
        + pool(weights[:, 0, 1], from_above)
        + pool(weights[:, 0, 2], far_y)
        + pool(weights[:, 0, 3], from_below)
        + pool(weights[:, 1, 0], side_x)
        + pool(weights[:, 1, 1], side_above)
        + pool(weights[:, 1, 2], side_far)
        + pool(weights[:, 1, 3], side_below)
    ).astype(jnp.bfloat16)
    pooled = pooled.reshape(local_blocks, term_total, row_count, width_two)
    right_done = jnp.einsum(
        "ktrn,tmn->ktrm", pooled, right_factor, preferred_element_type=jnp.float32
    ).astype(jnp.bfloat16)
    left_part = lax.dynamic_slice_in_dim(left_factor, part * row_count, row_count, axis=2)
    rates_run = left_rates[None]
    rates_parts = lax.all_to_all(
        jnp.broadcast_to(rates_run, (pieces,) + left_rates.shape), "sub", 0, 0, tiled=True
    )
    rates_full = jnp.moveaxis(rates_parts, 0, 1).reshape(local_blocks, width_two)
    partial = jnp.einsum(
        "tab,ktbc->kac", left_part, right_done, preferred_element_type=jnp.float32
    ).astype(jnp.bfloat16)
    dual_cols = jnp.einsum(
        "jab,jbc->jac", left_dual, partial, preferred_element_type=jnp.float32
    ).astype(jnp.bfloat16)
    mixed = jnp.einsum("jrn,jmn->jrm", dual_cols, right_dual, preferred_element_type=jnp.float32)
    scaled = (mixed / (rates_full[:, :, None] + right_rates[:, None, :])).astype(jnp.bfloat16)
    basis_rows = jnp.einsum(
        "jrm,jkm->jrk", scaled, right_eigenvector_matrix, preferred_element_type=jnp.float32
    ).astype(jnp.bfloat16)

    def make_chunk(idx):
        piece = lax.dynamic_slice_in_dim(basis_rows, idx * cols, cols, axis=2)
        return jnp.einsum(
            "jab,jbc->jac", left_basis, piece, preferred_element_type=jnp.float32
        ).astype(jnp.bfloat16)

    return scatter_sum(make_chunk, pieces, "sub")


def solution(mesh):
    placed = (
        P("blk", "sub", None),
        P(),
        P(),
        P(),
        P(),
        P("blk", None, None),
        P("blk", None, None),
        P("blk", None, None),
        P("blk", None, None),
        P("blk", "sub"),
        P("blk", None),
    )
    return jax.shard_map(
        local, mesh=mesh, in_specs=placed, out_specs=P("blk", None, "sub"), check_vma=False
    )
```
